32 devices in a mesh: gx: 8 (over z, x), gy: 4 (over y, core).
Axes of the slice: x: 2, y: 2, z: 4, core: 2. Of those that a mesh axis runs over, the one named last changes fastest.
Arguments:
- adjoint: float32 [3, 128, 64, 128], P(None, 'gx', 'gy'), may hold values from -4 to 4
- base_flow: float32 [3, 128, 64, 128], P(None, 'gx', 'gy'), may hold values from -4 to 4
- metric: float32 [64], P('gy'), may hold values from 0.1 to 1
- smoothing: float32 [64], P('gy'), may hold values from 1.5 to 16
Outputs:
- adjoint_next: float32 [3, 128, 64, 128], P(None, 'gx', 'gy')
- wall_gradient: float32 [2, 128, 128], P(None, 'gx')
The draws below stay inside these ranges and needn't reach their ends.
All inputs are finite; a program needn't handle non-finite values.
Results may differ from the reference program's by a relative error of at most 0.000071.
Values sent between devices are 32-bit elements; how exact they have to be, the bound alone decides.
No kernel may reach another device: no remote copies, remote signals or barrier semaphores. Data moves between devices by JAX's collectives and lax.ppermute only.
A program may use at most 64 MiB of HBM per device.

```python
import math
import jax
import jax.numpy as jnp
from jax import lax

CX = 16
NZ = 128
NX = 128
NY = 64


def draw_adjoint(key, part):
    array_shape = (3, NX, NY, NZ)
    values = jnp.clip(jax.random.normal(key, array_shape, jnp.float32), -4.0, 4.0)
    return values


def shard_levels(own_key, dims, cuts, low, high):
    gain, own = 1.0, jax.random.fold_in(own_key, 6)
    for axis_at, parts in cuts:
        steps = jnp.exp(jax.random.uniform(jax.random.fold_in(own, axis_at), (parts,), jnp.float32, low / len(cuts), high / len(cuts)))
        gain = gain * jnp.repeat(steps, dims[axis_at] // parts).reshape([-1 if axis == axis_at else 1 for axis in range(len(dims))])
    return gain


def noise(rng, shape, spread, reach, split=(), dtype=jnp.bfloat16):
    loudness = shard_levels(rng, shape, split, -0.22, 0.18) if split else 1.0
    result = jax.random.normal(rng, shape, jnp.float32) * spread * loudness
    return jnp.minimum(jnp.maximum(result, -reach), reach).astype(dtype)


def setup_inputs(seed: int = 0) -> dict:
    streams_of = jax.random.split(jax.random.key(seed), 5)
    adjoint = draw_adjoint(jax.random.fold_in(streams_of[4], 71), 0)
    base_flow = noise(streams_of[1], (3, NX, NY, NZ), 1.0, 4.0, ((1, 8), (2, 4)), jnp.float32)
    metric = jnp.clip(jnp.exp(math.log(1.0) - 2.3025851 * jax.random.uniform(streams_of[2], (NY,), jnp.float32) ** shard_levels(streams_of[2], (NY,), ((0, 4),), -0.2, 0.2)), 0.1, 1.0)
    smoothing = jnp.clip(jnp.exp(math.log(16.0) - 2.3671236 * jax.random.uniform(streams_of[3], (NY,), jnp.float32) ** shard_levels(streams_of[3], (NY,), ((0, 4),), -0.2, 0.2)), 1.5, 16.0)
    return dict(adjoint=adjoint, base_flow=base_flow, metric=metric, smoothing=smoothing)


step_size = 0.5
highest = lax.Precision.HIGHEST


def derivative(padded, metric, direction):
    if direction == 0:
        return 0.5 * (padded[2:, 1:-1] - padded[:-2, 1:-1])
    if direction == 1:
        return metric[None, :, None] * (padded[1:-1, 2:] - padded[1:-1, :-2])
    center = padded[1:-1, 1:-1]
    return 0.5 * (jnp.roll(center, -1, axis=2) - jnp.roll(center, 1, axis=2))


def advect(padded_adjoint, padded_base, adjoint, base_flow, metric):
    results = []
    for component in range(3):
        running = jnp.zeros(adjoint.shape[1:], jnp.float32)
        for direction in range(3):
            running = running - base_flow[direction] * derivative(padded_adjoint[component], metric, direction)
            running = running + adjoint[direction] * derivative(padded_base[direction], metric, component)
        results.append(step_size * running)
    return jnp.stack(results)


def reference(adjoint, base_flow, metric, smoothing):
    widths = ((1, 1), (1, 1), (0, 0))
    padded_adjoint = [jnp.pad(adjoint[component], widths) for component in range(3)]
    padded_base = [jnp.pad(base_flow[component], widths) for component in range(3)]
    increment = advect(padded_adjoint, padded_base, adjoint, base_flow, metric)
    decay_rate = 1.0 / (CX * smoothing)
    decay = jnp.exp(-decay_rate)[None, :, None]
    along_x = jnp.moveaxis(increment, 1, 0)

    def sweep_step(running_sum, column):
        running_sum = column + decay * running_sum
        return running_sum, running_sum

    start = jnp.zeros((3, NY, NZ), jnp.float32)
    final_carry, forward = lax.scan(sweep_step, start, along_x)
    final_back, backward = lax.scan(sweep_step, start, forward, reverse=True)
    shrink = jnp.expm1(-decay_rate) ** 2
    adjoint_next = adjoint + shrink[None, None, :, None] * jnp.moveaxis(backward, 0, 1)
    inverse = 1.0 / metric
    weighted = jnp.einsum('xyz,y->xz', adjoint_next[0], inverse, precision=highest)
    bulk_mean = weighted / jnp.sum(inverse)
    lower_wall = 2.0 * metric[0] * adjoint_next[1, :, 0, :] + bulk_mean
    upper_wall = -2.0 * metric[-1] * adjoint_next[1, :, -1, :] + bulk_mean
    return adjoint_next, jnp.stack([lower_wall, upper_wall])
```

```python
import jax
import jax.numpy as jnp
from jax import lax
from jax.sharding import PartitionSpec as P

step_size = 0.5
highest = lax.Precision.HIGHEST
CX = 16
DIRECT_LIMIT = 8


def shift(x, axis, size, step):
    if step > 0:
        pairs = [(j, j + step) for j in range(size - step)]
    else:
        pairs = [(j - step, j) for j in range(size + step)]
    return lax.ppermute(x, axis, pairs)


def halo(f, halves, dim):
    lo, hi = halves
    return (
        jnp.concatenate([lo, lax.slice_in_dim(f, 0, f.shape[dim] - 1, axis=dim)], axis=dim),
        jnp.concatenate([lax.slice_in_dim(f, 1, f.shape[dim], axis=dim), hi], axis=dim),
    )


def increments(adjoint, base_flow, xh, yh, metric):
    m = metric[None, :, None]
    nb = 3

    def diffs(k, f):
        bx, ax = xh[0][k], xh[1][k]
        by, ay = yh[0][k], yh[1][k]
        prev_x, next_x = halo(f, (bx, ax), 0)
        prev_y, next_y = halo(f, (by, ay), 1)
        dx = 0.5 * (next_x - prev_x)
        dy = m * (next_y - prev_y)
        dz = 0.5 * (jnp.roll(f, -1, axis=2) - jnp.roll(f, 1, axis=2))
        return (dx, dy, dz)

    d_adj = [diffs(c, adjoint[c]) for c in range(3)]
    d_base = [diffs(nb + d, base_flow[d]) for d in range(3)]
    results = []
    for c in range(3):
        running = jnp.zeros(adjoint.shape[1:], jnp.float32)
        for d in range(3):
            running = running - base_flow[d] * d_adj[c][d]
            running = running + adjoint[d] * d_base[d][c]
        results.append(step_size * running)
    return jnp.stack(results)


def gx_carries(L, U, A, G, i):
    if G <= DIRECT_LIMIT:
        payload = jnp.stack([L, U])
        inflow = jnp.zeros_like(L)
        ret = jnp.zeros_like(U)
        for k in range(1, G):
            got = lax.ppermute(payload, "gx", [(j, (j + k) % G) for j in range(G)])
            upstream = i >= k
            w_up = A ** (k - 1)
            w_down = A ** (G - k - 1)
            inflow = inflow + jnp.where(upstream, w_up * got[0], 0.0)
            ret = ret + jnp.where(upstream, 0.0, w_down * got[1])
        return inflow, ret
    inflow = shift(L, "gx", G, 1)
    ret = shift(U, "gx", G, -1)
    step = 1
    ratio = A
    while step < G:
        inflow = inflow + ratio * shift(inflow, "gx", G, step)
        ret = ret + ratio * shift(ret, "gx", G, -step)
        ratio = ratio * ratio
        step *= 2
    return inflow, ret


def local(adjoint, base_flow, metric, smoothing):
    G, i = lax.axis_size("gx"), lax.axis_index("gx")
    Gy, g = lax.axis_size("gy"), lax.axis_index("gy")
    n = adjoint.shape[1]

    x_lo = jnp.concatenate([adjoint[:, :1], base_flow[:, :1]])
    x_hi = jnp.concatenate([adjoint[:, -1:], base_flow[:, -1:]])
    y_lo = jnp.concatenate([adjoint[:, :, :1], base_flow[:, :, :1]])
    y_hi = jnp.concatenate([adjoint[:, :, -1:], base_flow[:, :, -1:]])
    xh = (shift(x_hi, "gx", G, 1), shift(x_lo, "gx", G, -1))
    yh = (shift(y_hi, "gy", Gy, 1), shift(y_lo, "gy", Gy, -1))

    increment = increments(adjoint, base_flow, xh, yh, metric)

    rate = 1.0 / (CX * smoothing)
    positions = jnp.arange(n, dtype=jnp.float32)
    offsets = positions[:, None] - positions[None, :]
    powers = jnp.where(
        offsets[None] >= 0.0,
        jnp.exp(-jnp.maximum(offsets, 0.0)[None] * rate[:, None, None]),
        0.0,
    )
    local_forward = jnp.einsum("jik,ckjz->cijz", powers, increment, precision=highest)
    local_back = jnp.einsum("jki,ckjz->cijz", powers, local_forward, precision=highest)

    A = jnp.exp(-n * rate)[None, :, None]
    lead = jnp.exp(-(positions[:, None] + 1.0) * rate[None, :])
    tail = jnp.exp(-(n - positions[:, None]) * rate[None, :])
    back_lead = jnp.einsum("jki,kj->ij", powers, lead, precision=highest)
    c = back_lead[0][None, :, None]
    two_block = jnp.expm1(-2.0 * n * rate)[None, :, None]

    def geo(m):
        return jnp.expm1(-2.0 * n * m * rate)[None, :, None] / two_block

    L = local_forward[:, -1]
    S = local_back[:, 0]
    downstream = (G - 1 - i).astype(jnp.float32)
    geo_here = geo(downstream)
    U = S + c * A * geo_here * L
    inflow, R = gx_carries(L, U, A, G, i)
    ret = R + c * geo_here * (L + A * inflow)

    swept = (
        local_back
        + back_lead[None, :, :, None] * inflow[:, None]
        + tail[None, :, :, None] * ret[:, None]
    )
    shrink = jnp.expm1(-rate) ** 2
    adjoint_next = adjoint + shrink[None, None, :, None] * swept

    lower_wall = jnp.where(g == 0, 2.0 * metric[0] * adjoint_next[1, :, 0, :], 0.0)
    upper_wall = jnp.where(g == Gy - 1, -2.0 * metric[-1] * adjoint_next[1, :, -1, :], 0.0)
    inverse = 1.0 / metric
    weighted = jnp.einsum("xjz,j->xz", adjoint_next[0], inverse, precision=highest)
    total_inv = jnp.broadcast_to(jnp.sum(inverse), weighted.shape)
    part = jnp.stack([lower_wall, upper_wall, weighted, total_inv])
    pieces = [part] + [
        lax.ppermute(part, "gy", [(j, (j + k) % Gy) for j in range(Gy)]) for k in range(1, Gy)
    ]
    stacked = jnp.stack(pieces)
    total = None
    for s in range(Gy):
        piece = lax.dynamic_index_in_dim(stacked, (g - s) % Gy, axis=0, keepdims=False)
        total = piece if total is None else total + piece
    bulk_mean = total[2] / total[3]
    wall_gradient = total[:2] + bulk_mean[None]
    return (adjoint_next, wall_gradient)


def solution(mesh):
    in_specs = (P(None, "gx", "gy", None), P(None, "gx", "gy", None), P("gy"), P("gy"))
    out_specs = (P(None, "gx", "gy", None), P(None, "gx", None))
    return jax.shard_map(local, mesh=mesh, in_specs=in_specs, out_specs=out_specs, check_vma=False)
```

```python
import functools
import jax
import jax.numpy as jnp
from jax import lax
from jax.experimental import pallas as pl
from jax.experimental.pallas import tpu as pltpu
from jax.sharding import PartitionSpec as P

step_size = 0.5
CX = 16
DIRECT_LIMIT = 8


def shift(x, axis, size, step):
    if step > 0:
        pairs = [(j, j + step) for j in range(size - step)]
    else:
        pairs = [(j - step, j) for j in range(size + step)]
    return lax.ppermute(x, axis, pairs)


def f32(shape):
    return jax.ShapeDtypeStruct(shape, jnp.float32)


def edges_kernel(adj_ref, base_ref, xlo_ref, xhi_ref, ylo_ref, yhi_ref):
    n, ny = adj_ref.shape[1], adj_ref.shape[2]
    for k in range(6):
        ref, c = (adj_ref, k) if k < 3 else (base_ref, k - 3)
        xlo_ref[k] = ref[c, 0]
        xhi_ref[k] = ref[c, n - 1]
        for x in range(n):
            ylo_ref[k, x : x + 1, :] = ref[c, x, 0:1, :]
            yhi_ref[k, x : x + 1, :] = ref[c, x, ny - 1 : ny, :]


def sweep_kernel(adj_ref, base_ref, xlo_ref, xhi_ref, ylo_ref, yhi_ref, coef_ref, sw_ref, pay_ref):
    n, ny, nz = adj_ref.shape[1], adj_ref.shape[2], adj_ref.shape[3]
    metric = coef_ref[0]
    decay = coef_ref[1]
    gain = coef_ref[2]
    row = lax.broadcasted_iota(jnp.int32, (ny, nz), 0)

    def field(k, x):
        if x < 0:
            return xlo_ref[k]
        if x >= n:
            return xhi_ref[k]
        return adj_ref[k, x] if k < 3 else base_ref[k - 3, x]

    forward = [None] * 3
    for x in range(n):
        grads = []
        for k in range(6):
            cur = field(k, x)
            dx = 0.5 * (field(k, x + 1) - field(k, x - 1))
            up = jnp.where(row == ny - 1, yhi_ref[k, x : x + 1, :], pltpu.roll(cur, ny - 1, 0))
            down = jnp.where(row == 0, ylo_ref[k, x : x + 1, :], pltpu.roll(cur, 1, 0))
            dy = metric * (up - down)
            dz = 0.5 * (pltpu.roll(cur, nz - 1, 1) - pltpu.roll(cur, 1, 1))
            grads.append((dx, dy, dz))
        adj = [field(d, x) for d in range(3)]
        base = [field(3 + d, x) for d in range(3)]
        for c in range(3):
            running = None
            for d in range(3):
                term = -(base[d] * grads[c][d])
                running = term if running is None else running + term
                running = running + adj[d] * grads[3 + d][c]
            inc = step_size * running
            forward[c] = inc if x == 0 else inc + decay * forward[c]
            sw_ref[c, x] = forward[c]
    back = [None] * 3
    for x in range(n - 1, -1, -1):
        for c in range(3):
            f = sw_ref[c, x]
            back[c] = f if x == n - 1 else f + decay * back[c]
            sw_ref[c, x] = back[c]
    for c in range(3):
        pay_ref[0, c] = forward[c]
        pay_ref[1, c] = back[c] + gain * forward[c]


def finish_kernel(adj_ref, sw_ref, pay_ref, inflow_ref, rest_ref, coef_ref, out_ref, part_ref):
    n, ny = adj_ref.shape[1], adj_ref.shape[2]
    rate = coef_ref[0]
    decay = coef_ref[1]
    shrink = coef_ref[2]
    inverse = coef_ref[3]
    low_w = coef_ref[4]
    high_w = coef_ref[5]
    near = coef_ref[6]
    ratio = coef_ref[7]
    ret = [rest_ref[c] + near * (pay_ref[0, c] + ratio * inflow_ref[c]) for c in range(3)]
    inflow = [inflow_ref[c] for c in range(3)]
    back_lead = None
    for x in range(n - 1, -1, -1):
        lead = jnp.exp(-(x + 1.0) * rate)
        back_lead = lead if back_lead is None else lead + decay * back_lead
        tail = jnp.exp(-(n - x) * rate)
        vals = []
        for c in range(3):
            v = adj_ref[c, x] + shrink * (sw_ref[c, x] + back_lead * inflow[c] + tail * ret[c])
            out_ref[c, x] = v
            vals.append(v)
        part_ref[0, x : x + 1, :] = (low_w * vals[1])[0:1, :]
        part_ref[1, x : x + 1, :] = (high_w * vals[1])[ny - 1 : ny, :]
        part_ref[2, x : x + 1, :] = jnp.sum(vals[0] * inverse, axis=0, keepdims=True)
    part_ref[3] = jnp.broadcast_to(jnp.sum(inverse, axis=0, keepdims=True), part_ref.shape[1:])


def gx_carries(L, U, A, G, i):
    if G <= DIRECT_LIMIT:
        payload = jnp.stack([L, U])
        inflow = jnp.zeros_like(L)
        ret = jnp.zeros_like(U)
        for k in range(1, G):
            got = lax.ppermute(payload, "gx", [(j, (j + k) % G) for j in range(G)])
            upstream = i >= k
            inflow = inflow + jnp.where(upstream, A ** (k - 1) * got[0], 0.0)
            ret = ret + jnp.where(upstream, 0.0, A ** (G - k - 1) * got[1])
        return inflow, ret
    inflow = shift(L, "gx", G, 1)
    ret = shift(U, "gx", G, -1)
    step = 1
    ratio = A
    while step < G:
        inflow = inflow + ratio * shift(inflow, "gx", G, step)
        ret = ret + ratio * shift(ret, "gx", G, -step)
        ratio = ratio * ratio
        step *= 2
    return inflow, ret


def local(adjoint, base_flow, metric, smoothing):
    G, i = lax.axis_size("gx"), lax.axis_index("gx")
    Gy, g = lax.axis_size("gy"), lax.axis_index("gy")
    _, n, ny, nz = adjoint.shape

    xlo, xhi, ylo, yhi = pl.pallas_call(
        edges_kernel,
        out_shape=(f32((6, ny, nz)), f32((6, ny, nz)), f32((6, n, nz)), f32((6, n, nz))),
    )(adjoint, base_flow)
    x_before = shift(xhi, "gx", G, 1)
    x_after = shift(xlo, "gx", G, -1)
    y_before = shift(yhi, "gy", Gy, 1)
    y_after = shift(ylo, "gy", Gy, -1)

    rate = 1.0 / (CX * smoothing)
    decay = jnp.exp(-rate)
    A = jnp.exp(-n * rate)
    c = jnp.sum(jnp.exp(-(2.0 * jnp.arange(n, dtype=jnp.float32)[:, None] + 1.0) * rate[None, :]), axis=0)
    two_block = jnp.expm1(-2.0 * n * rate)
    downstream = (G - 1 - i).astype(jnp.float32)
    geo_here = jnp.expm1(-2.0 * n * downstream * rate) / two_block

    def rows(*vs):
        return jnp.broadcast_to(jnp.stack(vs)[:, :, None], (len(vs), ny, nz))

    coef_a = rows(metric, decay, c * A * geo_here)
    sw, payload = pl.pallas_call(
        sweep_kernel,
        out_shape=(f32(adjoint.shape), f32((2, 3, ny, nz))),
    )(adjoint, base_flow, x_before, x_after, y_before, y_after, coef_a)

    A3 = A[None, :, None]
    inflow, rest = gx_carries(payload[0], payload[1], A3, G, i)

    low_w = jnp.where(g == 0, 2.0 * metric[0], 0.0) + jnp.zeros_like(metric)
    high_w = jnp.where(g == Gy - 1, -2.0 * metric[-1], 0.0) + jnp.zeros_like(metric)
    coef_b = rows(rate, decay, jnp.expm1(-rate) ** 2, 1.0 / metric, low_w, high_w, c * geo_here, A)
    adjoint_next, part = pl.pallas_call(
        finish_kernel,
        out_shape=(f32(adjoint.shape), f32((4, n, nz))),
    )(adjoint, sw, payload, inflow, rest, coef_b)

    pieces = [part] + [
        lax.ppermute(part, "gy", [(j, (j + k) % Gy) for j in range(Gy)]) for k in range(1, Gy)
    ]
    stacked = jnp.stack(pieces)
    total = None
    for s in range(Gy):
        piece = lax.dynamic_index_in_dim(stacked, (g - s) % Gy, axis=0, keepdims=False)
        total = piece if total is None else total + piece
    bulk_mean = total[2] / total[3]
    wall_gradient = total[:2] + bulk_mean[None]
    return (adjoint_next, wall_gradient)


def solution(mesh):
    in_specs = (P(None, "gx", "gy", None), P(None, "gx", "gy", None), P("gy"), P("gy"))
    out_specs = (P(None, "gx", "gy", None), P(None, "gx", None))
    return jax.shard_map(local, mesh=mesh, in_specs=in_specs, out_specs=out_specs, check_vma=False)
```

```python
import jax
import jax.numpy as jnp
from jax import lax
from jax.experimental import pallas as pl
from jax.experimental.pallas import tpu as pltpu
from jax.sharding import PartitionSpec as P

step_size = 0.5
CX = 16
DIRECT_LIMIT = 8


def shift(x, axis, size, step):
    if step > 0:
        pairs = [(j, j + step) for j in range(size - step)]
    else:
        pairs = [(j - step, j) for j in range(size + step)]
    return lax.ppermute(x, axis, pairs)


def f32(shape):
    return jax.ShapeDtypeStruct(shape, jnp.float32)


ANY = pl.BlockSpec(memory_space=pl.ANY)
SMEM = pl.BlockSpec(memory_space=pltpu.SMEM)


def edges_kernel(adj_ref, base_ref, xlo_ref, xhi_ref, ylo_ref, yhi_ref, sems):
    n, ny = adj_ref.shape[1], adj_ref.shape[2]
    copies = []
    for s, src in enumerate((adj_ref, base_ref)):
        dst = pl.ds(3 * s, 3)
        copies += [
            pltpu.make_async_copy(src.at[:, 0], xlo_ref.at[dst], sems.at[4 * s]),
            pltpu.make_async_copy(src.at[:, n - 1], xhi_ref.at[dst], sems.at[4 * s + 1]),
            pltpu.make_async_copy(src.at[:, :, 0], ylo_ref.at[dst], sems.at[4 * s + 2]),
            pltpu.make_async_copy(src.at[:, :, ny - 1], yhi_ref.at[dst], sems.at[4 * s + 3]),
        ]
    for cp in copies:
        cp.start()
    for cp in copies:
        cp.wait()


def sweep_kernel(G, direct, idx_ref, adj_ref, base_ref, xlo_ref, xhi_ref, ylo_ref, yhi_ref, coef_ref, sw_ref, own_ref, *send_refs):
    n, ny, nz = adj_ref.shape[1], adj_ref.shape[2], adj_ref.shape[3]
    metric = coef_ref[0]
    decay = coef_ref[1]
    gain = coef_ref[2]
    row = lax.broadcasted_iota(jnp.int32, (ny, nz), 0)

    def field(k, x):
        if x < 0:
            return xlo_ref[k]
        if x >= n:
            return xhi_ref[k]
        return adj_ref[k, x] if k < 3 else base_ref[k - 3, x]

    forward = [None] * 3
    for x in range(n):
        grads = []
        for k in range(6):
            cur = field(k, x)
            dx = 0.5 * (field(k, x + 1) - field(k, x - 1))
            up = jnp.where(row == ny - 1, yhi_ref[k, x : x + 1, :], pltpu.roll(cur, ny - 1, 0))
            down = jnp.where(row == 0, ylo_ref[k, x : x + 1, :], pltpu.roll(cur, 1, 0))
            dy = metric * (up - down)
            dz = 0.5 * (pltpu.roll(cur, nz - 1, 1) - pltpu.roll(cur, 1, 1))
            grads.append((dx, dy, dz))
        adj = [field(d, x) for d in range(3)]
        base = [field(3 + d, x) for d in range(3)]
        for c in range(3):
            running = None
            for d in range(3):
                term = -(base[d] * grads[c][d])
                running = term if running is None else running + term
                running = running + adj[d] * grads[3 + d][c]
            inc = step_size * running
            forward[c] = inc if x == 0 else inc + decay * forward[c]
            sw_ref[c, x] = forward[c]
    back = [None] * 3
    for x in range(n - 1, -1, -1):
        for c in range(3):
            f = sw_ref[c, x]
            back[c] = f if x == n - 1 else f + decay * back[c]
            sw_ref[c, x] = back[c]
    i = idx_ref[0]
    for c in range(3):
        carry_up = forward[c]
        carry_down = back[c] + gain * forward[c]
        own_ref[0, c] = carry_up
        own_ref[1, c] = carry_down
        if direct:
            for k in range(1, G):
                send_refs[k - 1][c] = jnp.where(i + k < G, carry_up, carry_down)


def finish_kernel(G, direct, idx_ref, adj_ref, sw_ref, own_ref, coef_ref, *rest):
    n, ny = adj_ref.shape[1], adj_ref.shape[2]
    out_ref, part_ref = rest[-2], rest[-1]
    got = rest[:-2]
    rate = coef_ref[3]
    decay = coef_ref[1]
    shrink = coef_ref[4]
    inverse = coef_ref[5]
    low_w = coef_ref[6]
    high_w = coef_ref[7]
    near = coef_ref[8]
    ratio = coef_ref[9]
    block_rate = n * rate
    i = idx_ref[0]
    inflow, later = [], []
    for c in range(3):
        if direct:
            a = jnp.zeros_like(rate)
            b = jnp.zeros_like(rate)
            for k in range(1, G):
                upstream = i >= k
                power = jnp.where(upstream, k - 1, G - k - 1).astype(jnp.float32)
                term = jnp.exp(-power * block_rate) * got[k - 1][c]
                a = a + jnp.where(upstream, term, 0.0)
                b = b + jnp.where(upstream, 0.0, term)
        else:
            a = got[0][c]
            b = got[1][c]
        inflow.append(a)
        later.append(b + near * (own_ref[0, c] + ratio * a))
    back_lead = None
    for x in range(n - 1, -1, -1):
        lead = jnp.exp(-(x + 1.0) * rate)
        back_lead = lead if back_lead is None else lead + decay * back_lead
        tail = jnp.exp(-(n - x) * rate)
        vals = []
        for c in range(3):
            v = adj_ref[c, x] + shrink * (sw_ref[c, x] + back_lead * inflow[c] + tail * later[c])
            out_ref[c, x] = v
            vals.append(v)
        part_ref[0, x : x + 1, :] = (low_w * vals[1])[0:1, :]
        part_ref[1, x : x + 1, :] = (high_w * vals[1])[ny - 1 : ny, :]
        part_ref[2, x : x + 1, :] = jnp.sum(vals[0] * inverse, axis=0, keepdims=True)
    part_ref[3] = jnp.broadcast_to(jnp.sum(inverse, axis=0, keepdims=True), part_ref.shape[1:])


def scan_carries(L, U, A, G):
    inflow = shift(L, "gx", G, 1)
    later = shift(U, "gx", G, -1)
    step = 1
    ratio = A
    while step < G:
        inflow = inflow + ratio * shift(inflow, "gx", G, step)
        later = later + ratio * shift(later, "gx", G, -step)
        ratio = ratio * ratio
        step *= 2
    return inflow, later


def local(adjoint, base_flow, metric, smoothing):
    G, i = lax.axis_size("gx"), lax.axis_index("gx")
    Gy, g = lax.axis_size("gy"), lax.axis_index("gy")
    _, n, ny, nz = adjoint.shape
    direct = G <= DIRECT_LIMIT
    idx = jnp.reshape(i, (1,)).astype(jnp.int32)

    xlo, xhi, ylo, yhi = pl.pallas_call(
        edges_kernel,
        out_shape=(f32((6, ny, nz)), f32((6, ny, nz)), f32((6, n, nz)), f32((6, n, nz))),
        in_specs=[ANY, ANY],
        out_specs=(ANY, ANY, ANY, ANY),
        scratch_shapes=[pltpu.SemaphoreType.DMA((8,))],
    )(adjoint, base_flow)
    x_before = shift(xhi, "gx", G, 1)
    x_after = shift(xlo, "gx", G, -1)
    y_before = shift(yhi, "gy", Gy, 1)
    y_after = shift(ylo, "gy", Gy, -1)

    rate = 1.0 / (CX * smoothing)
    decay = jnp.exp(-rate)
    A = jnp.exp(-n * rate)
    c = jnp.sum(jnp.exp(-(2.0 * jnp.arange(n, dtype=jnp.float32)[:, None] + 1.0) * rate[None, :]), axis=0)
    two_block = jnp.expm1(-2.0 * n * rate)
    downstream = (G - 1 - i).astype(jnp.float32)
    geo_here = jnp.expm1(-2.0 * n * downstream * rate) / two_block
    low_w = jnp.where(g == 0, 2.0 * metric[0], 0.0) + jnp.zeros_like(metric)
    high_w = jnp.where(g == Gy - 1, -2.0 * metric[-1], 0.0) + jnp.zeros_like(metric)
    vs = (metric, decay, c * A * geo_here, rate, jnp.expm1(-rate) ** 2, 1.0 / metric, low_w, high_w, c * geo_here, A)
    coef = jnp.broadcast_to(jnp.stack(vs)[:, :, None], (len(vs), ny, nz))

    plane = f32((3, ny, nz))
    sends = G - 1 if direct else 0
    outs = pl.pallas_call(
        lambda *r: sweep_kernel(G, direct, *r),
        out_shape=(f32(adjoint.shape), f32((2, 3, ny, nz))) + (plane,) * sends,
        in_specs=[SMEM] + [pl.BlockSpec(memory_space=pltpu.VMEM)] * 7,
    )(idx, adjoint, base_flow, x_before, x_after, y_before, y_after, coef)
    sw, own = outs[0], outs[1]

    if direct:
        got = [
            lax.ppermute(outs[1 + k], "gx", [(j, (j + k) % G) for j in range(G)]) for k in range(1, G)
        ]
    else:
        got = list(scan_carries(own[0], own[1], A[None, :, None], G))

    adjoint_next, part = pl.pallas_call(
        lambda *r: finish_kernel(G, direct, *r),
        out_shape=(f32(adjoint.shape), f32((4, n, nz))),
        in_specs=[SMEM] + [pl.BlockSpec(memory_space=pltpu.VMEM)] * (4 + len(got)),
    )(idx, adjoint, sw, own, coef, *got)

    pieces = [part] + [
        lax.ppermute(part, "gy", [(j, (j + k) % Gy) for j in range(Gy)]) for k in range(1, Gy)
    ]
    stacked = jnp.stack(pieces)
    total = None
    for s in range(Gy):
        piece = lax.dynamic_index_in_dim(stacked, (g - s) % Gy, axis=0, keepdims=False)
        total = piece if total is None else total + piece
    bulk_mean = total[2] / total[3]
    wall_gradient = total[:2] + bulk_mean[None]
    return (adjoint_next, wall_gradient)


def solution(mesh):
    in_specs = (P(None, "gx", "gy", None), P(None, "gx", "gy", None), P("gy"), P("gy"))
    out_specs = (P(None, "gx", "gy", None), P(None, "gx", None))
    return jax.shard_map(local, mesh=mesh, in_specs=in_specs, out_specs=out_specs, check_vma=False)
```

```python
import jax
import jax.numpy as jnp
from jax import lax
from jax.experimental import pallas as pl
from jax.experimental.pallas import tpu as pltpu
from jax.sharding import PartitionSpec as P

step_size = 0.5
CX = 16
DIRECT_LIMIT = 8


def shift(x, axis, size, step):
    if step > 0:
        pairs = [(j, j + step) for j in range(size - step)]
    else:
        pairs = [(j - step, j) for j in range(size + step)]
    return lax.ppermute(x, axis, pairs)


def f32(shape):
    return jax.ShapeDtypeStruct(shape, jnp.float32)


ANY = pl.BlockSpec(memory_space=pl.ANY)
SMEM = pl.BlockSpec(memory_space=pltpu.SMEM)


def column(ref, k, ny, nz):
    return jnp.broadcast_to(ref[:, k : k + 1], (ny, nz))


def edges_kernel(adj_ref, base_ref, xlo_ref, xhi_ref, ylo_ref, yhi_ref):
    n, ny = adj_ref.shape[1], adj_ref.shape[2]
    for k in range(6):
        ref, c = (adj_ref, k) if k < 3 else (base_ref, k - 3)
        xlo_ref[k] = ref[c, 0]
        xhi_ref[k] = ref[c, n - 1]
        for x in range(n):
            ylo_ref[k, x : x + 1, :] = ref[c, x, 0:1, :]
            yhi_ref[k, x : x + 1, :] = ref[c, x, ny - 1 : ny, :]


def sweep_kernel(G, direct, idx_ref, adj_ref, base_ref, xlo_ref, xhi_ref, ylo_ref, yhi_ref, coef_ref, sw_ref, own_ref, *send_refs):
    n, ny, nz = adj_ref.shape[1], adj_ref.shape[2], adj_ref.shape[3]
    metric = column(coef_ref, 0, ny, nz)
    decay = column(coef_ref, 1, ny, nz)
    gain = column(coef_ref, 2, ny, nz)
    row = lax.broadcasted_iota(jnp.int32, (ny, nz), 0)

    def field(k, x):
        if x < 0:
            return xlo_ref[k]
        if x >= n:
            return xhi_ref[k]
        return adj_ref[k, x] if k < 3 else base_ref[k - 3, x]

    forward = [None] * 3
    for x in range(n):
        grads = []
        for k in range(6):
            cur = field(k, x)
            dx = 0.5 * (field(k, x + 1) - field(k, x - 1))
            up = jnp.where(row == ny - 1, yhi_ref[k, x : x + 1, :], pltpu.roll(cur, ny - 1, 0))
            down = jnp.where(row == 0, ylo_ref[k, x : x + 1, :], pltpu.roll(cur, 1, 0))
            dy = metric * (up - down)
            dz = 0.5 * (pltpu.roll(cur, nz - 1, 1) - pltpu.roll(cur, 1, 1))
            grads.append((dx, dy, dz))
        adj = [field(d, x) for d in range(3)]
        base = [field(3 + d, x) for d in range(3)]
        for c in range(3):
            running = None
            for d in range(3):
                term = -(base[d] * grads[c][d])
                running = term if running is None else running + term
                running = running + adj[d] * grads[3 + d][c]
            inc = step_size * running
            forward[c] = inc if x == 0 else inc + decay * forward[c]
            sw_ref[c, x] = forward[c]
    back = [None] * 3
    for x in range(n - 1, -1, -1):
        for c in range(3):
            f = sw_ref[c, x]
            back[c] = f if x == n - 1 else f + decay * back[c]
            sw_ref[c, x] = back[c]
    for c in range(3):
        carry_up = forward[c]
        carry_down = back[c] + gain * forward[c]
        own_ref[0, c] = carry_up
        own_ref[1, c] = carry_down
        if direct:
            for k in range(1, G):
                send_refs[k - 1][c] = jnp.where(idx_ref[k] > 0, carry_up, carry_down)


def finish_kernel(G, direct, idx_ref, adj_ref, sw_ref, own_ref, coef_ref, *rest):
    n, ny = adj_ref.shape[1], adj_ref.shape[2]
    out_ref, part_ref = rest[-2], rest[-1]
    got = rest[:-2]
    nz = adj_ref.shape[3]
    rate = column(coef_ref, 3, ny, nz)
    decay = column(coef_ref, 1, ny, nz)
    shrink = column(coef_ref, 4, ny, nz)
    inverse = column(coef_ref, 5, ny, nz)
    low_w = column(coef_ref, 6, ny, nz)
    high_w = column(coef_ref, 7, ny, nz)
    near = column(coef_ref, 8, ny, nz)
    ratio = column(coef_ref, 9, ny, nz)
    block_rate = n * rate
    inflow, later = [], []
    for c in range(3):
        if direct:
            a = jnp.zeros_like(rate)
            b = jnp.zeros_like(rate)
            for k in range(1, G):
                upstream = idx_ref[k] == 0
                power = idx_ref[G - 1 + k].astype(jnp.float32)
                term = jnp.exp(-power * block_rate) * got[k - 1][c]
                a = a + jnp.where(upstream, term, 0.0)
                b = b + jnp.where(upstream, 0.0, term)
        else:
            a = got[0][c]
            b = got[1][c]
        inflow.append(a)
        later.append(b + near * (own_ref[0, c] + ratio * a))
    back_lead = None
    for x in range(n - 1, -1, -1):
        lead = jnp.exp(-(x + 1.0) * rate)
        back_lead = lead if back_lead is None else lead + decay * back_lead
        tail = jnp.exp(-(n - x) * rate)
        vals = []
        for c in range(3):
            v = adj_ref[c, x] + shrink * (sw_ref[c, x] + back_lead * inflow[c] + tail * later[c])
            out_ref[c, x] = v
            vals.append(v)
        part_ref[0, x : x + 1, :] = (low_w * vals[1])[0:1, :]
        part_ref[1, x : x + 1, :] = (high_w * vals[1])[ny - 1 : ny, :]
        part_ref[2, x : x + 1, :] = jnp.sum(vals[0] * inverse, axis=0, keepdims=True)
    part_ref[3] = jnp.broadcast_to(jnp.sum(inverse, axis=0, keepdims=True), part_ref.shape[1:])


def is_pow2(size):
    return size & (size - 1) == 0


def partner_of(j, k, size):
    if is_pow2(size):
        return j ^ k
    return (j + k) % size


def slot_of(g, s, size):
    if is_pow2(size):
        return g ^ s
    return (g - s) % size


def scan_carries(L, U, A, G):
    inflow = shift(L, "gx", G, 1)
    later = shift(U, "gx", G, -1)
    step = 1
    ratio = A
    while step < G:
        inflow = inflow + ratio * shift(inflow, "gx", G, step)
        later = later + ratio * shift(later, "gx", G, -step)
        ratio = ratio * ratio
        step *= 2
    return inflow, later


def local(adjoint, base_flow, metric, smoothing):
    G, i = lax.axis_size("gx"), lax.axis_index("gx")
    Gy, g = lax.axis_size("gy"), lax.axis_index("gy")
    _, n, ny, nz = adjoint.shape
    direct = G <= DIRECT_LIMIT and is_pow2(G)
    partner = [partner_of(i, k, G) for k in range(1, G)] if direct else []
    sends_up = [(p > i).astype(jnp.int32) for p in partner]
    powers = [jnp.abs(p - i).astype(jnp.int32) - 1 for p in partner]
    idx = jnp.stack([jnp.asarray(i, jnp.int32)] + sends_up + powers)

    xlo, xhi, ylo, yhi = pl.pallas_call(
        edges_kernel,
        out_shape=(f32((6, ny, nz)), f32((6, ny, nz)), f32((6, n, nz)), f32((6, n, nz))),
    )(adjoint, base_flow)
    x_before = shift(xhi, "gx", G, 1)
    x_after = shift(xlo, "gx", G, -1)
    y_before = shift(yhi, "gy", Gy, 1)
    y_after = shift(ylo, "gy", Gy, -1)

    rate = 1.0 / (CX * smoothing)
    decay = jnp.exp(-rate)
    A = jnp.exp(-n * rate)
    c = jnp.sum(jnp.exp(-(2.0 * jnp.arange(n, dtype=jnp.float32)[:, None] + 1.0) * rate[None, :]), axis=0)
    two_block = jnp.expm1(-2.0 * n * rate)
    downstream = (G - 1 - i).astype(jnp.float32)
    geo_here = jnp.expm1(-2.0 * n * downstream * rate) / two_block
    low_w = jnp.where(g == 0, 2.0 * metric[0], 0.0) + jnp.zeros_like(metric)
    high_w = jnp.where(g == Gy - 1, -2.0 * metric[-1], 0.0) + jnp.zeros_like(metric)
    vs = (metric, decay, c * A * geo_here, rate, jnp.expm1(-rate) ** 2, 1.0 / metric, low_w, high_w, c * geo_here, A)
    coef = jnp.stack(vs, axis=1)

    plane = f32((3, ny, nz))
    sends = G - 1 if direct else 0
    outs = pl.pallas_call(
        lambda *r: sweep_kernel(G, direct, *r),
        out_shape=(f32(adjoint.shape), f32((2, 3, ny, nz))) + (plane,) * sends,
        in_specs=[SMEM] + [pl.BlockSpec(memory_space=pltpu.VMEM)] * 7,
    )(idx, adjoint, base_flow, x_before, x_after, y_before, y_after, coef)
    sw, own = outs[0], outs[1]

    if direct:
        got = [
            lax.ppermute(outs[1 + k], "gx", [(j, partner_of(j, k, G)) for j in range(G)])
            for k in range(1, G)
        ]
    else:
        got = list(scan_carries(own[0], own[1], A[None, :, None], G))

    adjoint_next, part = pl.pallas_call(
        lambda *r: finish_kernel(G, direct, *r),
        out_shape=(f32(adjoint.shape), f32((4, n, nz))),
        in_specs=[SMEM] + [pl.BlockSpec(memory_space=pltpu.VMEM)] * (4 + len(got)),
    )(idx, adjoint, sw, own, coef, *got)

    pieces = [part] + [
        lax.ppermute(part, "gy", [(j, partner_of(j, k, Gy)) for j in range(Gy)]) for k in range(1, Gy)
    ]
    stacked = jnp.stack(pieces)
    total = None
    for s in range(Gy):
        piece = lax.dynamic_index_in_dim(stacked, slot_of(g, s, Gy), axis=0, keepdims=False)
        total = piece if total is None else total + piece
    bulk_mean = total[2] / total[3]
    wall_gradient = total[:2] + bulk_mean[None]
    return (adjoint_next, wall_gradient)


def solution(mesh):
    in_specs = (P(None, "gx", "gy", None), P(None, "gx", "gy", None), P("gy"), P("gy"))
    out_specs = (P(None, "gx", "gy", None), P(None, "gx", None))
    return jax.shard_map(local, mesh=mesh, in_specs=in_specs, out_specs=out_specs, check_vma=False)
```

```python
import jax
import jax.numpy as jnp
from jax import lax
from jax.experimental import pallas as pl
from jax.experimental.pallas import tpu as pltpu
from jax.sharding import PartitionSpec as P

step_size = 0.5
CX = 16
DIRECT_LIMIT = 8


def shift(x, axis, size, step):
    if step > 0:
        pairs = [(j, j + step) for j in range(size - step)]
    else:
        pairs = [(j - step, j) for j in range(size + step)]
    return lax.ppermute(x, axis, pairs)


def f32(shape):
    return jax.ShapeDtypeStruct(shape, jnp.float32)


def column(ref, k, ny, nz):
    return jnp.broadcast_to(ref[:, k : k + 1], (ny, nz))


def is_pow2(size):
    return size & (size - 1) == 0


def partner_of(j, k, size):
    if is_pow2(size):
        return j ^ k
    return (j + k) % size


def slot_of(g, s, size):
    if is_pow2(size):
        return g ^ s
    return (g - s) % size


def edges_kernel(adj_ref, base_ref, xlo_ref, xhi_ref, ylo_ref, yhi_ref):
    n, ny = adj_ref.shape[1], adj_ref.shape[2]
    for k in range(6):
        ref, c = (adj_ref, k) if k < 3 else (base_ref, k - 3)
        xlo_ref[k] = ref[c, 0]
        xhi_ref[k] = ref[c, n - 1]
        for x in range(n):
            ylo_ref[k, x : x + 1, :] = ref[c, x, 0:1, :]
            yhi_ref[k, x : x + 1, :] = ref[c, x, ny - 1 : ny, :]


def sweep_kernel(adj_ref, base_ref, xlo_ref, xhi_ref, ylo_ref, yhi_ref, coef_ref, sw_ref, pay_ref):
    n, ny, nz = adj_ref.shape[1], adj_ref.shape[2], adj_ref.shape[3]
    metric = column(coef_ref, 0, ny, nz)
    decay = column(coef_ref, 1, ny, nz)
    gain = column(coef_ref, 2, ny, nz)
    row = lax.broadcasted_iota(jnp.int32, (ny, nz), 0)

    def field(k, x):
        if x < 0:
            return xlo_ref[k]
        if x >= n:
            return xhi_ref[k]
        return adj_ref[k, x] if k < 3 else base_ref[k - 3, x]

    forward = [None] * 3
    for x in range(n):
        grads = []
        for k in range(6):
            cur = field(k, x)
            dx = 0.5 * (field(k, x + 1) - field(k, x - 1))
            up = jnp.where(row == ny - 1, yhi_ref[k, x : x + 1, :], pltpu.roll(cur, ny - 1, 0))
            down = jnp.where(row == 0, ylo_ref[k, x : x + 1, :], pltpu.roll(cur, 1, 0))
            dy = metric * (up - down)
            dz = 0.5 * (pltpu.roll(cur, nz - 1, 1) - pltpu.roll(cur, 1, 1))
            grads.append((dx, dy, dz))
        adj = [field(d, x) for d in range(3)]
        base = [field(3 + d, x) for d in range(3)]
        for c in range(3):
            running = None
            for d in range(3):
                term = -(base[d] * grads[c][d])
                running = term if running is None else running + term
                running = running + adj[d] * grads[3 + d][c]
            inc = step_size * running
            forward[c] = inc if x == 0 else inc + decay * forward[c]
            sw_ref[c, x] = forward[c]
    back = [None] * 3
    for x in range(n - 1, -1, -1):
        for c in range(3):
            f = sw_ref[c, x]
            back[c] = f if x == n - 1 else f + decay * back[c]
            sw_ref[c, x] = back[c]
    for c in range(3):
        pay_ref[0, c] = forward[c]
        pay_ref[1, c] = back[c] + gain * forward[c]


def finish_kernel(G, direct, idx_ref, adj_ref, sw_ref, pay_ref, coef_ref, *rest):
    n, ny, nz = adj_ref.shape[1], adj_ref.shape[2], adj_ref.shape[3]
    out_ref, part_ref = rest[-2], rest[-1]
    got = rest[:-2]
    rate = column(coef_ref, 3, ny, nz)
    decay = column(coef_ref, 1, ny, nz)
    shrink = column(coef_ref, 4, ny, nz)
    inverse = column(coef_ref, 5, ny, nz)
    low_w = column(coef_ref, 6, ny, nz)
    high_w = column(coef_ref, 7, ny, nz)
    near = column(coef_ref, 8, ny, nz)
    ratio = column(coef_ref, 9, ny, nz)
    block_rate = n * rate
    i = idx_ref[0]
    inflow, later = [], []
    if direct:
        weights = []
        for k in range(1, G):
            j = lax.bitwise_xor(i, jnp.int32(k))
            upstream = j < i
            power = (jnp.maximum(i - j, j - i) - 1).astype(jnp.float32)
            weights.append((upstream, jnp.exp(-power * block_rate)))
    for c in range(3):
        if direct:
            a = jnp.zeros_like(rate)
            b = jnp.zeros_like(rate)
            for k in range(1, G):
                upstream, w = weights[k - 1]
                a = a + jnp.where(upstream, w * got[k - 1][0, c], 0.0)
                b = b + jnp.where(upstream, 0.0, w * got[k - 1][1, c])
        else:
            a = got[0][c]
            b = got[1][c]
        inflow.append(a)
        later.append(b + near * (pay_ref[0, c] + ratio * a))
    back_lead = None
    for x in range(n - 1, -1, -1):
        lead = jnp.exp(-(x + 1.0) * rate)
        back_lead = lead if back_lead is None else lead + decay * back_lead
        tail = jnp.exp(-(n - x) * rate)
        vals = []
        for c in range(3):
            v = adj_ref[c, x] + shrink * (sw_ref[c, x] + back_lead * inflow[c] + tail * later[c])
            out_ref[c, x] = v
            vals.append(v)
        part_ref[0, x : x + 1, :] = (low_w * vals[1])[0:1, :]
        part_ref[1, x : x + 1, :] = (high_w * vals[1])[ny - 1 : ny, :]
        part_ref[2, x : x + 1, :] = jnp.sum(vals[0] * inverse, axis=0, keepdims=True)
    part_ref[3] = jnp.broadcast_to(jnp.sum(inverse, axis=0, keepdims=True), part_ref.shape[1:])


def scan_carries(L, U, A, G):
    inflow = shift(L, "gx", G, 1)
    later = shift(U, "gx", G, -1)
    step = 1
    ratio = A
    while step < G:
        inflow = inflow + ratio * shift(inflow, "gx", G, step)
        later = later + ratio * shift(later, "gx", G, -step)
        ratio = ratio * ratio
        step *= 2
    return inflow, later


def local(adjoint, base_flow, metric, smoothing):
    G, i = lax.axis_size("gx"), lax.axis_index("gx")
    Gy, g = lax.axis_size("gy"), lax.axis_index("gy")
    _, n, ny, nz = adjoint.shape

    xlo, xhi, ylo, yhi = pl.pallas_call(
        edges_kernel,
        out_shape=(f32((6, ny, nz)), f32((6, ny, nz)), f32((6, n, nz)), f32((6, n, nz))),
    )(adjoint, base_flow)
    x_before = shift(xhi, "gx", G, 1)
    x_after = shift(xlo, "gx", G, -1)
    y_before = shift(yhi, "gy", Gy, 1)
    y_after = shift(ylo, "gy", Gy, -1)

    rate = 1.0 / (CX * smoothing)
    decay = jnp.exp(-rate)
    A = jnp.exp(-n * rate)
    c = jnp.sum(jnp.exp(-(2.0 * jnp.arange(n, dtype=jnp.float32)[:, None] + 1.0) * rate[None, :]), axis=0)
    two_block = jnp.expm1(-2.0 * n * rate)
    downstream = (G - 1 - i).astype(jnp.float32)
    geo_here = jnp.expm1(-2.0 * n * downstream * rate) / two_block

    low_w = jnp.where(g == 0, 2.0 * metric[0], 0.0) + jnp.zeros_like(metric)
    high_w = jnp.where(g == Gy - 1, -2.0 * metric[-1], 0.0) + jnp.zeros_like(metric)
    vs = (metric, decay, c * A * geo_here, rate, jnp.expm1(-rate) ** 2, 1.0 / metric, low_w, high_w, c * geo_here, A)
    coef = jnp.stack(vs, axis=1)
    sw, payload = pl.pallas_call(
        sweep_kernel,
        out_shape=(f32(adjoint.shape), f32((2, 3, ny, nz))),
    )(adjoint, base_flow, x_before, x_after, y_before, y_after, coef)

    direct = G <= DIRECT_LIMIT and is_pow2(G)
    if direct:
        got = [lax.ppermute(payload, "gx", [(j, j ^ k) for j in range(G)]) for k in range(1, G)]
    else:
        got = list(scan_carries(payload[0], payload[1], A[None, :, None], G))
    idx = jnp.reshape(i, (1,)).astype(jnp.int32)
    nvm = 4 + len(got)
    adjoint_next, part = pl.pallas_call(
        lambda *r: finish_kernel(G, direct, *r),
        out_shape=(f32(adjoint.shape), f32((4, n, nz))),
        in_specs=[pl.BlockSpec(memory_space=pltpu.SMEM)] + [pl.BlockSpec()] * nvm,
    )(idx, adjoint, sw, payload, coef, *got)

    pieces = [part] + [
        lax.ppermute(part, "gy", [(j, partner_of(j, k, Gy)) for j in range(Gy)]) for k in range(1, Gy)
    ]
    stacked = jnp.stack(pieces)
    total = None
    for s in range(Gy):
        piece = lax.dynamic_index_in_dim(stacked, slot_of(g, s, Gy), axis=0, keepdims=False)
        total = piece if total is None else total + piece
    bulk_mean = total[2] / total[3]
    wall_gradient = total[:2] + bulk_mean[None]
    return (adjoint_next, wall_gradient)


def solution(mesh):
    in_specs = (P(None, "gx", "gy", None), P(None, "gx", "gy", None), P("gy"), P("gy"))
    out_specs = (P(None, "gx", "gy", None), P(None, "gx", None))
    return jax.shard_map(local, mesh=mesh, in_specs=in_specs, out_specs=out_specs, check_vma=False)
```

```python
import jax
import jax.numpy as jnp
from jax import lax
from jax.experimental import pallas as pl
from jax.experimental.pallas import tpu as pltpu
from jax.sharding import PartitionSpec as P

step_size = 0.5
CX = 16
DIRECT_LIMIT = 8


def shift(x, axis, size, step):
    if step > 0:
        pairs = [(j, j + step) for j in range(size - step)]
    else:
        pairs = [(j - step, j) for j in range(size + step)]
    return lax.ppermute(x, axis, pairs)


def f32(shape):
    return jax.ShapeDtypeStruct(shape, jnp.float32)


def column(ref, k, ny, nz):
    return ref[k]


def is_pow2(size):
    return size & (size - 1) == 0


def partner_of(j, k, size):
    if is_pow2(size):
        return j ^ k
    return (j + k) % size


def slot_of(g, s, size):
    if is_pow2(size):
        return g ^ s
    return (g - s) % size


def expm1(x):
    t = jnp.ones_like(x)
    for k in range(12, 1, -1):
        t = 1.0 + x * t / k
    return jnp.where(jnp.abs(x) < 0.5, x * t, jnp.exp(x) - 1.0)


def edges_kernel(metric_ref, smooth_ref, adj_ref, base_ref, xlo_ref, xhi_ref, ylo_ref, yhi_ref, coef_ref):
    n, ny, nz = adj_ref.shape[1], adj_ref.shape[2], adj_ref.shape[3]
    for k in range(6):
        ref, c = (adj_ref, k) if k < 3 else (base_ref, k - 3)
        xlo_ref[k] = ref[c, 0]
        xhi_ref[k] = ref[c, n - 1]
        for x in range(n):
            ylo_ref[k, x : x + 1, :] = ref[c, x, 0:1, :]
            yhi_ref[k, x : x + 1, :] = ref[c, x, ny - 1 : ny, :]
    G, i = lax.axis_size("gx"), lax.axis_index("gx")
    Gy, g = lax.axis_size("gy"), lax.axis_index("gy")
    row = lax.broadcasted_iota(jnp.int32, (ny, nz), 0)
    metric = jnp.zeros((ny, nz), jnp.float32)
    smooth = jnp.zeros((ny, nz), jnp.float32)
    for y in range(ny):
        metric = jnp.where(row == y, metric_ref[y], metric)
        smooth = jnp.where(row == y, smooth_ref[y], smooth)
    rate = 1.0 / (CX * smooth)
    decay = jnp.exp(-rate)
    ratio = jnp.exp(-n * rate)
    c = None
    for k in range(n):
        term = jnp.exp(-(2.0 * k + 1.0) * rate)
        c = term if c is None else c + term
    downstream = (G - 1 - i).astype(jnp.float32)
    geo_here = expm1(-2.0 * n * downstream * rate) / expm1(-2.0 * n * rate)
    low = jnp.where(g == 0, 2.0 * metric_ref[0], 0.0)
    high = jnp.where(g == Gy - 1, -2.0 * metric_ref[ny - 1], 0.0)
    shrink = expm1(-rate)
    rows = (metric, decay, c * ratio * geo_here, rate, shrink * shrink, 1.0 / metric,
            jnp.broadcast_to(low, (ny, nz)), jnp.broadcast_to(high, (ny, nz)), c * geo_here, ratio)
    for k, v in enumerate(rows):
        coef_ref[k] = v


def sweep_kernel(adj_ref, base_ref, xlo_ref, xhi_ref, ylo_ref, yhi_ref, coef_ref, sw_ref, pay_ref):
    n, ny, nz = adj_ref.shape[1], adj_ref.shape[2], adj_ref.shape[3]
    metric = column(coef_ref, 0, ny, nz)
    decay = column(coef_ref, 1, ny, nz)
    gain = column(coef_ref, 2, ny, nz)
    row = lax.broadcasted_iota(jnp.int32, (ny, nz), 0)

    def field(k, x):
        if x < 0:
            return xlo_ref[k]
        if x >= n:
            return xhi_ref[k]
        return adj_ref[k, x] if k < 3 else base_ref[k - 3, x]

    forward = [None] * 3
    for x in range(n):
        grads = []
        for k in range(6):
            cur = field(k, x)
            dx = 0.5 * (field(k, x + 1) - field(k, x - 1))
            up = jnp.where(row == ny - 1, yhi_ref[k, x : x + 1, :], pltpu.roll(cur, ny - 1, 0))
            down = jnp.where(row == 0, ylo_ref[k, x : x + 1, :], pltpu.roll(cur, 1, 0))
            dy = metric * (up - down)
            dz = 0.5 * (pltpu.roll(cur, nz - 1, 1) - pltpu.roll(cur, 1, 1))
            grads.append((dx, dy, dz))
        adj = [field(d, x) for d in range(3)]
        base = [field(3 + d, x) for d in range(3)]
        for c in range(3):
            running = None
            for d in range(3):
                term = -(base[d] * grads[c][d])
                running = term if running is None else running + term
                running = running + adj[d] * grads[3 + d][c]
            inc = step_size * running
            forward[c] = inc if x == 0 else inc + decay * forward[c]
            sw_ref[c, x] = forward[c]
    back = [None] * 3
    for x in range(n - 1, -1, -1):
        for c in range(3):
            f = sw_ref[c, x]
            back[c] = f if x == n - 1 else f + decay * back[c]
            sw_ref[c, x] = back[c]
    for c in range(3):
        pay_ref[0, c] = forward[c]
        pay_ref[1, c] = back[c] + gain * forward[c]


def finish_kernel(G, direct, adj_ref, sw_ref, pay_ref, coef_ref, *rest):
    n, ny, nz = adj_ref.shape[1], adj_ref.shape[2], adj_ref.shape[3]
    out_ref, part_ref = rest[-2], rest[-1]
    got = rest[:-2]
    rate = column(coef_ref, 3, ny, nz)
    decay = column(coef_ref, 1, ny, nz)
    shrink = column(coef_ref, 4, ny, nz)
    inverse = column(coef_ref, 5, ny, nz)
    low_w = column(coef_ref, 6, ny, nz)
    high_w = column(coef_ref, 7, ny, nz)
    near = column(coef_ref, 8, ny, nz)
    ratio = column(coef_ref, 9, ny, nz)
    block_rate = n * rate
    i = lax.axis_index("gx")
    inflow, later = [], []
    if direct:
        weights = []
        for k in range(1, G):
            j = lax.bitwise_xor(i, jnp.int32(k))
            upstream = j < i
            power = (jnp.maximum(i - j, j - i) - 1).astype(jnp.float32)
            weights.append((upstream, jnp.exp(-power * block_rate)))
    for c in range(3):
        if direct:
            a = jnp.zeros_like(rate)
            b = jnp.zeros_like(rate)
            for k in range(1, G):
                upstream, w = weights[k - 1]
                a = a + jnp.where(upstream, w * got[k - 1][0, c], 0.0)
                b = b + jnp.where(upstream, 0.0, w * got[k - 1][1, c])
        else:
            a = got[0][c]
            b = got[1][c]
        inflow.append(a)
        later.append(b + near * (pay_ref[0, c] + ratio * a))
    back_lead = None
    for x in range(n - 1, -1, -1):
        lead = jnp.exp(-(x + 1.0) * rate)
        back_lead = lead if back_lead is None else lead + decay * back_lead
        tail = jnp.exp(-(n - x) * rate)
        vals = []
        for c in range(3):
            v = adj_ref[c, x] + shrink * (sw_ref[c, x] + back_lead * inflow[c] + tail * later[c])
            out_ref[c, x] = v
            vals.append(v)
        part_ref[0, x : x + 1, :] = (low_w * vals[1])[0:1, :]
        part_ref[1, x : x + 1, :] = (high_w * vals[1])[ny - 1 : ny, :]
        part_ref[2, x : x + 1, :] = jnp.sum(vals[0] * inverse, axis=0, keepdims=True)
    part_ref[3] = jnp.broadcast_to(jnp.sum(inverse, axis=0, keepdims=True), part_ref.shape[1:])


def scan_carries(L, U, A, G):
    inflow = shift(L, "gx", G, 1)
    later = shift(U, "gx", G, -1)
    step = 1
    ratio = A
    while step < G:
        inflow = inflow + ratio * shift(inflow, "gx", G, step)
        later = later + ratio * shift(later, "gx", G, -step)
        ratio = ratio * ratio
        step *= 2
    return inflow, later


def local(adjoint, base_flow, metric, smoothing):
    G, i = lax.axis_size("gx"), lax.axis_index("gx")
    Gy, g = lax.axis_size("gy"), lax.axis_index("gy")
    _, n, ny, nz = adjoint.shape

    smem = pl.BlockSpec(memory_space=pltpu.SMEM)
    xlo, xhi, ylo, yhi, coef = pl.pallas_call(
        edges_kernel,
        out_shape=(f32((6, ny, nz)), f32((6, ny, nz)), f32((6, n, nz)), f32((6, n, nz)), f32((10, ny, nz))),
        in_specs=[smem, smem, pl.BlockSpec(), pl.BlockSpec()],
    )(metric, smoothing, adjoint, base_flow)
    x_before = shift(xhi, "gx", G, 1)
    x_after = shift(xlo, "gx", G, -1)
    y_before = shift(yhi, "gy", Gy, 1)
    y_after = shift(ylo, "gy", Gy, -1)

    sw, payload = pl.pallas_call(
        sweep_kernel,
        out_shape=(f32(adjoint.shape), f32((2, 3, ny, nz))),
    )(adjoint, base_flow, x_before, x_after, y_before, y_after, coef)

    direct = G <= DIRECT_LIMIT and is_pow2(G)
    if direct:
        got = [lax.ppermute(payload, "gx", [(j, j ^ k) for j in range(G)]) for k in range(1, G)]
    else:
        A = coef[9]
        got = list(scan_carries(payload[0], payload[1], A[None], G))
    adjoint_next, part = pl.pallas_call(
        lambda *r: finish_kernel(G, direct, *r),
        out_shape=(f32(adjoint.shape), f32((4, n, nz))),
    )(adjoint, sw, payload, coef, *got)

    pieces = [part] + [
        lax.ppermute(part, "gy", [(j, (j + k) % Gy) for j in range(Gy)]) for k in range(1, Gy)
    ]
    stacked = jnp.stack(pieces)
    total = None
    for s in range(Gy):
        piece = lax.dynamic_index_in_dim(stacked, (g - s) % Gy, axis=0, keepdims=False)
        total = piece if total is None else total + piece
    bulk_mean = total[2] / total[3]
    wall_gradient = total[:2] + bulk_mean[None]
    return (adjoint_next, wall_gradient)


def solution(mesh):
    in_specs = (P(None, "gx", "gy", None), P(None, "gx", "gy", None), P("gy"), P("gy"))
    out_specs = (P(None, "gx", "gy", None), P(None, "gx", None))
    return jax.shard_map(local, mesh=mesh, in_specs=in_specs, out_specs=out_specs, check_vma=False)
```

```python
import jax
import jax.numpy as jnp
from jax import lax
from jax.experimental import pallas as pl
from jax.experimental.pallas import tpu as pltpu
from jax.sharding import PartitionSpec as P

step_size = 0.5
CX = 16
DIRECT_LIMIT = 8


def shift(x, axis, size, step):
    if step > 0:
        pairs = [(j, j + step) for j in range(size - step)]
    else:
        pairs = [(j - step, j) for j in range(size + step)]
    return lax.ppermute(x, axis, pairs)


def f32(shape):
    return jax.ShapeDtypeStruct(shape, jnp.float32)


def column(ref, k, ny, nz):
    return ref[k]


def is_pow2(size):
    return size & (size - 1) == 0


def partner_of(j, k, size):
    if is_pow2(size):
        return j ^ k
    return (j + k) % size


def slot_of(g, s, size):
    if is_pow2(size):
        return g ^ s
    return (g - s) % size


def expm1(x):
    t = jnp.ones_like(x)
    for k in range(12, 1, -1):
        t = 1.0 + x * t / k
    return jnp.where(jnp.abs(x) < 0.5, x * t, jnp.exp(x) - 1.0)


def edges_kernel(metric_ref, smooth_ref, adj_ref, base_ref, xlo_ref, xhi_ref, ylo_ref, yhi_ref, coef_ref):
    n, ny, nz = adj_ref.shape[1], adj_ref.shape[2], adj_ref.shape[3]
    for k in range(6):
        ref, c = (adj_ref, k) if k < 3 else (base_ref, k - 3)
        xlo_ref[k] = ref[c, 0]
        xhi_ref[k] = ref[c, n - 1]
        for x in range(n):
            ylo_ref[k, x : x + 1, :] = ref[c, x, 0:1, :]
            yhi_ref[k, x : x + 1, :] = ref[c, x, ny - 1 : ny, :]
    G, i = lax.axis_size("gx"), lax.axis_index("gx")
    Gy, g = lax.axis_size("gy"), lax.axis_index("gy")
    row = lax.broadcasted_iota(jnp.int32, (ny, nz), 0)
    metric = jnp.zeros((ny, nz), jnp.float32)
    smooth = jnp.zeros((ny, nz), jnp.float32)
    for y in range(ny):
        metric = jnp.where(row == y, metric_ref[y], metric)
        smooth = jnp.where(row == y, smooth_ref[y], smooth)
    rate = 1.0 / (CX * smooth)
    decay = jnp.exp(-rate)
    ratio = jnp.exp(-n * rate)
    c = None
    for k in range(n):
        term = jnp.exp(-(2.0 * k + 1.0) * rate)
        c = term if c is None else c + term
    downstream = (G - 1 - i).astype(jnp.float32)
    geo_here = expm1(-2.0 * n * downstream * rate) / expm1(-2.0 * n * rate)
    low = jnp.where(g == 0, 2.0 * metric_ref[0], 0.0)
    high = jnp.where(g == Gy - 1, -2.0 * metric_ref[ny - 1], 0.0)
    shrink = expm1(-rate)
    rows = (metric, decay, c * ratio * geo_here, rate, shrink * shrink, 1.0 / metric,
            jnp.broadcast_to(low, (ny, nz)), jnp.broadcast_to(high, (ny, nz)), c * geo_here, ratio)
    for k, v in enumerate(rows):
        coef_ref[k] = v


def sweep_kernel(adj_ref, base_ref, coef_ref, sw_ref, pay_ref):
    n, ny, nz = adj_ref.shape[1], adj_ref.shape[2], adj_ref.shape[3]
    metric = column(coef_ref, 0, ny, nz)
    decay = column(coef_ref, 1, ny, nz)
    row = lax.broadcasted_iota(jnp.int32, (ny, nz), 0)
    zero = jnp.zeros((ny, nz), jnp.float32)

    def field(k, x):
        if x < 0 or x >= n:
            return zero
        return adj_ref[k, x] if k < 3 else base_ref[k - 3, x]

    forward = [None] * 3
    for x in range(n):
        grads = []
        for k in range(6):
            cur = field(k, x)
            dx = 0.5 * (field(k, x + 1) - field(k, x - 1))
            up = jnp.where(row == ny - 1, 0.0, pltpu.roll(cur, ny - 1, 0))
            down = jnp.where(row == 0, 0.0, pltpu.roll(cur, 1, 0))
            dy = metric * (up - down)
            dz = 0.5 * (pltpu.roll(cur, nz - 1, 1) - pltpu.roll(cur, 1, 1))
            grads.append((dx, dy, dz))
        adj = [field(d, x) for d in range(3)]
        base = [field(3 + d, x) for d in range(3)]
        for c in range(3):
            running = None
            for d in range(3):
                term = -(base[d] * grads[c][d])
                running = term if running is None else running + term
                running = running + adj[d] * grads[3 + d][c]
            inc = step_size * running
            forward[c] = inc if x == 0 else inc + decay * forward[c]
            sw_ref[c, x] = forward[c]
    back = [None] * 3
    for x in range(n - 1, -1, -1):
        for c in range(3):
            f = sw_ref[c, x]
            back[c] = f if x == n - 1 else f + decay * back[c]
            sw_ref[c, x] = back[c]
    for c in range(3):
        pay_ref[0, c] = forward[c]
        pay_ref[1, c] = back[c]


def delta_terms(own, halo, scale, along):
    out = []
    for c in range(3):
        term = -(own[3 + along] * (scale * halo[c]))
        if c == along:
            for d in range(3):
                term = term + own[d] * (scale * halo[3 + d])
        out.append(step_size * term)
    return out


def edge_kernel(xlo_ref, xhi_ref, ylo_ref, yhi_ref, xb_ref, xa_ref, yb_ref, ya_ref, coef_ref, pre_ref,
                pay_ref, plane_ref, rows_ref):
    n, nz = ylo_ref.shape[1], ylo_ref.shape[2]
    ny = xlo_ref.shape[1]
    decay = column(coef_ref, 1, ny, nz)
    gain = column(coef_ref, 2, ny, nz)
    rate = column(coef_ref, 3, ny, nz)
    metric = column(coef_ref, 0, ny, nz)
    row = lax.broadcasted_iota(jnp.int32, (ny, nz), 0)
    first = delta_terms([xlo_ref[k] for k in range(6)], [xb_ref[k] for k in range(6)], -0.5, 0)
    last = delta_terms([xhi_ref[k] for k in range(6)], [xa_ref[k] for k in range(6)], 0.5, 0)
    low = delta_terms([ylo_ref[k] for k in range(6)], [yb_ref[k] for k in range(6)], -metric[0:1, :], 1)
    high = delta_terms([yhi_ref[k] for k in range(6)], [ya_ref[k] for k in range(6)], metric[ny - 1 : ny, :], 1)
    d_low = decay[0:1, :]
    d_high = decay[ny - 1 : ny, :]
    reach = jnp.exp(-(n - 1.0) * rate)
    spread = None
    for x in range(n - 1, -1, -1):
        lead = jnp.exp(-x * rate)
        spread = lead if spread is None else lead + decay * spread
    for c in range(3):
        plane_ref[0, c] = first[c]
        plane_ref[1, c] = last[c]
        f_lo = f_hi = None
        fl, fh = [], []
        for x in range(n):
            a = low[c][x : x + 1, :]
            b = high[c][x : x + 1, :]
            f_lo = a if f_lo is None else a + d_low * f_lo
            f_hi = b if f_hi is None else b + d_high * f_hi
            fl.append(f_lo)
            fh.append(f_hi)
        b_lo = b_hi = None
        for x in range(n - 1, -1, -1):
            b_lo = fl[x] if b_lo is None else fl[x] + d_low * b_lo
            b_hi = fh[x] if b_hi is None else fh[x] + d_high * b_hi
            rows_ref[c, 0, x : x + 1, :] = b_lo
            rows_ref[c, 1, x : x + 1, :] = b_hi
        row_l = jnp.where(row == 0, fl[n - 1], 0.0) + jnp.where(row == ny - 1, fh[n - 1], 0.0)
        row_s = jnp.where(row == 0, b_lo, 0.0) + jnp.where(row == ny - 1, b_hi, 0.0)
        carry_up = pre_ref[0, c] + reach * first[c] + last[c] + row_l
        start = pre_ref[1, c] + spread * first[c] + reach * last[c] + row_s
        pay_ref[0, c] = carry_up
        pay_ref[1, c] = start + gain * carry_up


def finish_kernel(G, direct, adj_ref, sw_ref, pay_ref, coef_ref, plane_ref, rows_ref, *rest):
    n, ny, nz = adj_ref.shape[1], adj_ref.shape[2], adj_ref.shape[3]
    out_ref, part_ref = rest[-2], rest[-1]
    got = rest[:-2]
    rate = column(coef_ref, 3, ny, nz)
    decay = column(coef_ref, 1, ny, nz)
    shrink = column(coef_ref, 4, ny, nz)
    inverse = column(coef_ref, 5, ny, nz)
    low_w = column(coef_ref, 6, ny, nz)
    high_w = column(coef_ref, 7, ny, nz)
    near = column(coef_ref, 8, ny, nz)
    ratio = column(coef_ref, 9, ny, nz)
    block_rate = n * rate
    i = lax.axis_index("gx")
    inflow, later = [], []
    if direct:
        weights = []
        for k in range(1, G):
            j = lax.bitwise_xor(i, jnp.int32(k))
            upstream = j < i
            power = (jnp.maximum(i - j, j - i) - 1).astype(jnp.float32)
            weights.append((upstream, jnp.exp(-power * block_rate)))
    for c in range(3):
        if direct:
            a = jnp.zeros_like(rate)
            b = jnp.zeros_like(rate)
            for k in range(1, G):
                upstream, w = weights[k - 1]
                a = a + jnp.where(upstream, w * got[k - 1][0, c], 0.0)
                b = b + jnp.where(upstream, 0.0, w * got[k - 1][1, c])
        else:
            a = got[0][c]
            b = got[1][c]
        inflow.append(a)
        later.append(b + near * (pay_ref[0, c] + ratio * a))
    row = lax.broadcasted_iota(jnp.int32, (ny, nz), 0)
    back_lead = None
    spread = None
    for x in range(n - 1, -1, -1):
        lead = jnp.exp(-(x + 1.0) * rate)
        back_lead = lead if back_lead is None else lead + decay * back_lead
        own_lead = jnp.exp(-x * rate)
        spread = own_lead if spread is None else own_lead + decay * spread
        tail = jnp.exp(-(n - x) * rate)
        reach = jnp.exp(-(n - 1.0 - x) * rate)
        vals = []
        for c in range(3):
            fix = jnp.where(row == 0, rows_ref[c, 0, x : x + 1, :], 0.0) + jnp.where(
                row == ny - 1, rows_ref[c, 1, x : x + 1, :], 0.0
            )
            local = sw_ref[c, x] + spread * plane_ref[0, c] + reach * plane_ref[1, c] + fix
            v = adj_ref[c, x] + shrink * (local + back_lead * inflow[c] + tail * later[c])
            out_ref[c, x] = v
            vals.append(v)
        part_ref[0, x : x + 1, :] = (low_w * vals[1])[0:1, :]
        part_ref[1, x : x + 1, :] = (high_w * vals[1])[ny - 1 : ny, :]
        part_ref[2, x : x + 1, :] = jnp.sum(vals[0] * inverse, axis=0, keepdims=True)
    part_ref[3] = jnp.broadcast_to(jnp.sum(inverse, axis=0, keepdims=True), part_ref.shape[1:])


def scan_carries(L, U, A, G):
    inflow = shift(L, "gx", G, 1)
    later = shift(U, "gx", G, -1)
    step = 1
    ratio = A
    while step < G:
        inflow = inflow + ratio * shift(inflow, "gx", G, step)
        later = later + ratio * shift(later, "gx", G, -step)
        ratio = ratio * ratio
        step *= 2
    return inflow, later


def local(adjoint, base_flow, metric, smoothing):
    G, i = lax.axis_size("gx"), lax.axis_index("gx")
    Gy, g = lax.axis_size("gy"), lax.axis_index("gy")
    _, n, ny, nz = adjoint.shape

    smem = pl.BlockSpec(memory_space=pltpu.SMEM)
    xlo, xhi, ylo, yhi, coef = pl.pallas_call(
        edges_kernel,
        out_shape=(f32((6, ny, nz)), f32((6, ny, nz)), f32((6, n, nz)), f32((6, n, nz)), f32((10, ny, nz))),
        in_specs=[smem, smem, pl.BlockSpec(), pl.BlockSpec()],
    )(metric, smoothing, adjoint, base_flow)
    x_before = shift(xhi, "gx", G, 1)
    x_after = shift(xlo, "gx", G, -1)
    y_before = shift(yhi, "gy", Gy, 1)
    y_after = shift(ylo, "gy", Gy, -1)

    sw, pre = pl.pallas_call(
        sweep_kernel,
        out_shape=(f32(adjoint.shape), f32((2, 3, ny, nz))),
    )(adjoint, base_flow, coef)
    payload, plane, rows = pl.pallas_call(
        edge_kernel,
        out_shape=(f32((2, 3, ny, nz)), f32((2, 3, ny, nz)), f32((3, 2, n, nz))),
    )(xlo, xhi, ylo, yhi, x_before, x_after, y_before, y_after, coef, pre)

    direct = G <= DIRECT_LIMIT and is_pow2(G)
    if direct:
        got = [lax.ppermute(payload, "gx", [(j, j ^ k) for j in range(G)]) for k in range(1, G)]
    else:
        A = coef[9]
        got = list(scan_carries(payload[0], payload[1], A[None], G))
    adjoint_next, part = pl.pallas_call(
        lambda *r: finish_kernel(G, direct, *r),
        out_shape=(f32(adjoint.shape), f32((4, n, nz))),
    )(adjoint, sw, payload, coef, plane, rows, *got)

    pieces = [part] + [
        lax.ppermute(part, "gy", [(j, (j + k) % Gy) for j in range(Gy)]) for k in range(1, Gy)
    ]
    stacked = jnp.stack(pieces)
    total = None
    for s in range(Gy):
        piece = lax.dynamic_index_in_dim(stacked, (g - s) % Gy, axis=0, keepdims=False)
        total = piece if total is None else total + piece
    bulk_mean = total[2] / total[3]
    wall_gradient = total[:2] + bulk_mean[None]
    return (adjoint_next, wall_gradient)


def solution(mesh):
    in_specs = (P(None, "gx", "gy", None), P(None, "gx", "gy", None), P("gy"), P("gy"))
    out_specs = (P(None, "gx", "gy", None), P(None, "gx", None))
    return jax.shard_map(local, mesh=mesh, in_specs=in_specs, out_specs=out_specs, check_vma=False)
```

```python
import jax
import jax.numpy as jnp
from jax import lax
from jax.experimental import pallas as pl
from jax.experimental.pallas import tpu as pltpu
from jax.sharding import PartitionSpec as P

step_size = 0.5
CX = 16
DIRECT_LIMIT = 8


def shift(x, axis, size, step):
    if step > 0:
        pairs = [(j, j + step) for j in range(size - step)]
    else:
        pairs = [(j - step, j) for j in range(size + step)]
    return lax.ppermute(x, axis, pairs)


def f32(shape):
    return jax.ShapeDtypeStruct(shape, jnp.float32)


def column(ref, k, ny, nz):
    return ref[k]


def is_pow2(size):
    return size & (size - 1) == 0


def partner_of(j, k, size):
    if is_pow2(size):
        return j ^ k
    return (j + k) % size


def slot_of(g, s, size):
    if is_pow2(size):
        return g ^ s
    return (g - s) % size


def expm1(x):
    t = jnp.ones_like(x)
    for k in range(12, 1, -1):
        t = 1.0 + x * t / k
    return jnp.where(jnp.abs(x) < 0.5, x * t, jnp.exp(x) - 1.0)


def edges_kernel(metric_ref, smooth_ref, adj_ref, base_ref, xlo_ref, xhi_ref, ylo_ref, yhi_ref, coef_ref):
    n, ny, nz = adj_ref.shape[1], adj_ref.shape[2], adj_ref.shape[3]
    for k in range(6):
        ref, c = (adj_ref, k) if k < 3 else (base_ref, k - 3)
        xlo_ref[k] = ref[c, 0]
        xhi_ref[k] = ref[c, n - 1]
        for x in range(n):
            ylo_ref[k, x : x + 1, :] = ref[c, x, 0:1, :]
            yhi_ref[k, x : x + 1, :] = ref[c, x, ny - 1 : ny, :]
    G, i = lax.axis_size("gx"), lax.axis_index("gx")
    Gy, g = lax.axis_size("gy"), lax.axis_index("gy")
    row = lax.broadcasted_iota(jnp.int32, (ny, nz), 0)
    metric = jnp.zeros((ny, nz), jnp.float32)
    smooth = jnp.zeros((ny, nz), jnp.float32)
    for y in range(ny):
        metric = jnp.where(row == y, metric_ref[y], metric)
        smooth = jnp.where(row == y, smooth_ref[y], smooth)
    rate = 1.0 / (CX * smooth)
    decay = jnp.exp(-rate)
    ratio = jnp.exp(-n * rate)
    c = None
    for k in range(n):
        term = jnp.exp(-(2.0 * k + 1.0) * rate)
        c = term if c is None else c + term
    downstream = (G - 1 - i).astype(jnp.float32)
    geo_here = expm1(-2.0 * n * downstream * rate) / expm1(-2.0 * n * rate)
    low = jnp.where(g == 0, 2.0 * metric_ref[0], 0.0)
    high = jnp.where(g == Gy - 1, -2.0 * metric_ref[ny - 1], 0.0)
    shrink = expm1(-rate)
    rows = (metric, decay, c * ratio * geo_here, rate, shrink * shrink, 1.0 / metric,
            jnp.broadcast_to(low, (ny, nz)), jnp.broadcast_to(high, (ny, nz)), c * geo_here, ratio)
    for k, v in enumerate(rows):
        coef_ref[k] = v


def sweep_kernel(adj_ref, base_ref, coef_ref, sw_ref, pay_ref):
    n, ny, nz = adj_ref.shape[1], adj_ref.shape[2], adj_ref.shape[3]
    metric = column(coef_ref, 0, ny, nz)
    decay = column(coef_ref, 1, ny, nz)
    row = lax.broadcasted_iota(jnp.int32, (ny, nz), 0)
    zero = jnp.zeros((ny, nz), jnp.float32)

    def field(k, x):
        if x < 0 or x >= n:
            return zero
        return adj_ref[k, x] if k < 3 else base_ref[k - 3, x]

    forward = [None] * 3
    for x in range(n):
        grads = []
        for k in range(6):
            cur = field(k, x)
            dx = 0.5 * (field(k, x + 1) - field(k, x - 1))
            up = jnp.where(row == ny - 1, 0.0, pltpu.roll(cur, ny - 1, 0))
            down = jnp.where(row == 0, 0.0, pltpu.roll(cur, 1, 0))
            dy = metric * (up - down)
            dz = 0.5 * (pltpu.roll(cur, nz - 1, 1) - pltpu.roll(cur, 1, 1))
            grads.append((dx, dy, dz))
        adj = [field(d, x) for d in range(3)]
        base = [field(3 + d, x) for d in range(3)]
        for c in range(3):
            running = None
            for d in range(3):
                term = -(base[d] * grads[c][d])
                running = term if running is None else running + term
                running = running + adj[d] * grads[3 + d][c]
            inc = step_size * running
            forward[c] = inc if x == 0 else inc + decay * forward[c]
            sw_ref[c, x] = forward[c]
    back = [None] * 3
    for x in range(n - 1, -1, -1):
        for c in range(3):
            f = sw_ref[c, x]
            back[c] = f if x == n - 1 else f + decay * back[c]
            sw_ref[c, x] = back[c]
    for c in range(3):
        pay_ref[0, c] = forward[c]
        pay_ref[1, c] = back[c]


def delta_terms(own, halo, scale, along):
    out = []
    for c in range(3):
        term = -(own[3 + along] * (scale * halo[c]))
        if c == along:
            for d in range(3):
                term = term + own[d] * (scale * halo[3 + d])
        out.append(step_size * term)
    return out


def edge_kernel(xlo_ref, xhi_ref, ylo_ref, yhi_ref, xb_ref, xa_ref, yb_ref, ya_ref, coef_ref, pre_ref,
                pay_ref, plane_ref, rows_ref):
    n, nz = ylo_ref.shape[1], ylo_ref.shape[2]
    ny = xlo_ref.shape[1]
    decay = column(coef_ref, 1, ny, nz)
    gain = column(coef_ref, 2, ny, nz)
    rate = column(coef_ref, 3, ny, nz)
    metric = column(coef_ref, 0, ny, nz)
    row = lax.broadcasted_iota(jnp.int32, (ny, nz), 0)
    first = delta_terms([xlo_ref[k] for k in range(6)], [xb_ref[k] for k in range(6)], -0.5, 0)
    last = delta_terms([xhi_ref[k] for k in range(6)], [xa_ref[k] for k in range(6)], 0.5, 0)
    low = delta_terms([ylo_ref[k] for k in range(6)], [yb_ref[k] for k in range(6)], -metric[0:1, :], 1)
    high = delta_terms([yhi_ref[k] for k in range(6)], [ya_ref[k] for k in range(6)], metric[ny - 1 : ny, :], 1)
    d_low = decay[0:1, :]
    d_high = decay[ny - 1 : ny, :]
    reach = jnp.exp(-(n - 1.0) * rate)
    spread = None
    for x in range(n - 1, -1, -1):
        lead = jnp.exp(-x * rate)
        spread = lead if spread is None else lead + decay * spread
    for c in range(3):
        plane_ref[0, c] = first[c]
        plane_ref[1, c] = last[c]
        f_lo = f_hi = None
        fl, fh = [], []
        for x in range(n):
            a = low[c][x : x + 1, :]
            b = high[c][x : x + 1, :]
            f_lo = a if f_lo is None else a + d_low * f_lo
            f_hi = b if f_hi is None else b + d_high * f_hi
            fl.append(f_lo)
            fh.append(f_hi)
        b_lo = b_hi = None
        for x in range(n - 1, -1, -1):
            b_lo = fl[x] if b_lo is None else fl[x] + d_low * b_lo
            b_hi = fh[x] if b_hi is None else fh[x] + d_high * b_hi
            rows_ref[c, 0, x : x + 1, :] = b_lo
            rows_ref[c, 1, x : x + 1, :] = b_hi
        row_l = jnp.where(row == 0, fl[n - 1], 0.0) + jnp.where(row == ny - 1, fh[n - 1], 0.0)
        row_s = jnp.where(row == 0, b_lo, 0.0) + jnp.where(row == ny - 1, b_hi, 0.0)
        carry_up = pre_ref[0, c] + reach * first[c] + last[c] + row_l
        start = pre_ref[1, c] + spread * first[c] + reach * last[c] + row_s
        pay_ref[0, c] = carry_up
        pay_ref[1, c] = start + gain * carry_up


def finish_kernel(G, direct, adj_ref, sw_ref, pay_ref, coef_ref, plane_ref, rows_ref, *rest):
    n, ny, nz = adj_ref.shape[1], adj_ref.shape[2], adj_ref.shape[3]
    out_ref, part_ref = rest[-2], rest[-1]
    got = rest[:-2]
    rate = column(coef_ref, 3, ny, nz)
    decay = column(coef_ref, 1, ny, nz)
    shrink = column(coef_ref, 4, ny, nz)
    inverse = column(coef_ref, 5, ny, nz)
    low_w = column(coef_ref, 6, ny, nz)
    high_w = column(coef_ref, 7, ny, nz)
    near = column(coef_ref, 8, ny, nz)
    ratio = column(coef_ref, 9, ny, nz)
    block_rate = n * rate
    i = lax.axis_index("gx")
    inflow, later = [], []
    if direct:
        pair_ref = got[0]
        far = got[1:]
        odd = (i % 2) == 1
        pair = i // 2
        step_w = jnp.exp(-block_rate)
        weights = []
        for m in range(1, G // 2):
            other = lax.bitwise_xor(pair, jnp.int32(m))
            upstream = other < pair
            power = (jnp.maximum(pair - other, other - pair) - 1).astype(jnp.float32)
            weights.append((upstream, jnp.exp(-2.0 * power * block_rate)))
    for c in range(3):
        if direct:
            a = jnp.zeros_like(rate)
            b = jnp.zeros_like(rate)
            for m in range(1, G // 2):
                upstream, w = weights[m - 1]
                a = a + jnp.where(upstream, w * far[m - 1][0, c], 0.0)
                b = b + jnp.where(upstream, 0.0, w * far[m - 1][1, c])
            a = jnp.where(odd, step_w * a + pair_ref[0, c], a)
            b = jnp.where(odd, b, pair_ref[1, c] + step_w * b)
        else:
            a = got[0][c]
            b = got[1][c]
        inflow.append(a)
        later.append(b + near * (pay_ref[0, c] + ratio * a))
    row = lax.broadcasted_iota(jnp.int32, (ny, nz), 0)
    back_lead = None
    spread = None
    for x in range(n - 1, -1, -1):
        lead = jnp.exp(-(x + 1.0) * rate)
        back_lead = lead if back_lead is None else lead + decay * back_lead
        own_lead = jnp.exp(-x * rate)
        spread = own_lead if spread is None else own_lead + decay * spread
        tail = jnp.exp(-(n - x) * rate)
        reach = jnp.exp(-(n - 1.0 - x) * rate)
        vals = []
        for c in range(3):
            fix = jnp.where(row == 0, rows_ref[c, 0, x : x + 1, :], 0.0) + jnp.where(
                row == ny - 1, rows_ref[c, 1, x : x + 1, :], 0.0
            )
            local = sw_ref[c, x] + spread * plane_ref[0, c] + reach * plane_ref[1, c] + fix
            v = adj_ref[c, x] + shrink * (local + back_lead * inflow[c] + tail * later[c])
            out_ref[c, x] = v
            vals.append(v)
        part_ref[0, x : x + 1, :] = (low_w * vals[1])[0:1, :]
        part_ref[1, x : x + 1, :] = (high_w * vals[1])[ny - 1 : ny, :]
        part_ref[2, x : x + 1, :] = jnp.sum(vals[0] * inverse, axis=0, keepdims=True)
    part_ref[3] = jnp.broadcast_to(jnp.sum(inverse, axis=0, keepdims=True), part_ref.shape[1:])


def scan_carries(L, U, A, G):
    inflow = shift(L, "gx", G, 1)
    later = shift(U, "gx", G, -1)
    step = 1
    ratio = A
    while step < G:
        inflow = inflow + ratio * shift(inflow, "gx", G, step)
        later = later + ratio * shift(later, "gx", G, -step)
        ratio = ratio * ratio
        step *= 2
    return inflow, later


def local(adjoint, base_flow, metric, smoothing):
    G, i = lax.axis_size("gx"), lax.axis_index("gx")
    Gy, g = lax.axis_size("gy"), lax.axis_index("gy")
    _, n, ny, nz = adjoint.shape

    smem = pl.BlockSpec(memory_space=pltpu.SMEM)
    xlo, xhi, ylo, yhi, coef = pl.pallas_call(
        edges_kernel,
        out_shape=(f32((6, ny, nz)), f32((6, ny, nz)), f32((6, n, nz)), f32((6, n, nz)), f32((10, ny, nz))),
        in_specs=[smem, smem, pl.BlockSpec(), pl.BlockSpec()],
    )(metric, smoothing, adjoint, base_flow)
    x_before = shift(xhi, "gx", G, 1)
    x_after = shift(xlo, "gx", G, -1)
    y_before = shift(yhi, "gy", Gy, 1)
    y_after = shift(ylo, "gy", Gy, -1)

    sw, pre = pl.pallas_call(
        sweep_kernel,
        out_shape=(f32(adjoint.shape), f32((2, 3, ny, nz))),
    )(adjoint, base_flow, coef)
    payload, plane, rows = pl.pallas_call(
        edge_kernel,
        out_shape=(f32((2, 3, ny, nz)), f32((2, 3, ny, nz)), f32((3, 2, n, nz))),
    )(xlo, xhi, ylo, yhi, x_before, x_after, y_before, y_after, coef, pre)

    direct = 2 <= G <= DIRECT_LIMIT and is_pow2(G)
    if direct:
        mate = lax.ppermute(payload, "gx", [(j, j ^ 1) for j in range(G)])
        odd = (i % 2) == 1
        A = coef[9][None]
        first_l = jnp.where(odd, mate[0], payload[0])
        second_l = jnp.where(odd, payload[0], mate[0])
        first_u = jnp.where(odd, mate[1], payload[1])
        second_u = jnp.where(odd, payload[1], mate[1])
        pair_sum = jnp.stack([A * first_l + second_l, first_u + A * second_u])
        got = [mate] + [
            lax.ppermute(pair_sum, "gx", [(j, j ^ (2 * m)) for j in range(G)]) for m in range(1, G // 2)
        ]
    else:
        A = coef[9]
        got = list(scan_carries(payload[0], payload[1], A[None], G))
    adjoint_next, part = pl.pallas_call(
        lambda *r: finish_kernel(G, direct, *r),
        out_shape=(f32(adjoint.shape), f32((4, n, nz))),
    )(adjoint, sw, payload, coef, plane, rows, *got)

    pieces = [part] + [
        lax.ppermute(part, "gy", [(j, (j + k) % Gy) for j in range(Gy)]) for k in range(1, Gy)
    ]
    stacked = jnp.stack(pieces)
    total = None
    for s in range(Gy):
        piece = lax.dynamic_index_in_dim(stacked, (g - s) % Gy, axis=0, keepdims=False)
        total = piece if total is None else total + piece
    bulk_mean = total[2] / total[3]
    wall_gradient = total[:2] + bulk_mean[None]
    return (adjoint_next, wall_gradient)


def solution(mesh):
    in_specs = (P(None, "gx", "gy", None), P(None, "gx", "gy", None), P("gy"), P("gy"))
    out_specs = (P(None, "gx", "gy", None), P(None, "gx", None))
    return jax.shard_map(local, mesh=mesh, in_specs=in_specs, out_specs=out_specs, check_vma=False)
```

```python
import jax
import jax.numpy as jnp
from jax import lax
from jax.experimental import pallas as pl
from jax.experimental.pallas import tpu as pltpu
from jax.sharding import PartitionSpec as P

step_size = 0.5
CX = 16
DIRECT_LIMIT = 8


def shift(x, axis, size, step):
    if step > 0:
        pairs = [(j, j + step) for j in range(size - step)]
    else:
        pairs = [(j - step, j) for j in range(size + step)]
    return lax.ppermute(x, axis, pairs)


def f32(shape):
    return jax.ShapeDtypeStruct(shape, jnp.float32)


def column(ref, k, ny, nz):
    return ref[k]


def is_pow2(size):
    return size & (size - 1) == 0


def partner_of(j, k, size):
    if is_pow2(size):
        return j ^ k
    return (j + k) % size


def slot_of(g, s, size):
    if is_pow2(size):
        return g ^ s
    return (g - s) % size


def expm1(x):
    t = jnp.ones_like(x)
    for k in range(12, 1, -1):
        t = 1.0 + x * t / k
    return jnp.where(jnp.abs(x) < 0.5, x * t, jnp.exp(x) - 1.0)


def edges_kernel(metric_ref, smooth_ref, adj_ref, base_ref, xa_ref, xb_ref, ya_ref, yb_ref, coef_ref):
    n, ny, nz = adj_ref.shape[1], adj_ref.shape[2], adj_ref.shape[3]
    even_x = lax.axis_index("gx") % 2 == 0
    even_y = lax.axis_index("gy") % 2 == 0
    for k in range(6):
        ref, c = (adj_ref, k) if k < 3 else (base_ref, k - 3)
        lo, hi = ref[c, 0], ref[c, n - 1]
        xa_ref[k] = jnp.where(even_x, hi, lo)
        xb_ref[k] = jnp.where(even_x, lo, hi)
        for x in range(n):
            lo, hi = ref[c, x, 0:1, :], ref[c, x, ny - 1 : ny, :]
            ya_ref[k, x : x + 1, :] = jnp.where(even_y, hi, lo)
            yb_ref[k, x : x + 1, :] = jnp.where(even_y, lo, hi)
    G, i = lax.axis_size("gx"), lax.axis_index("gx")
    Gy, g = lax.axis_size("gy"), lax.axis_index("gy")
    row = lax.broadcasted_iota(jnp.int32, (ny, nz), 0)
    metric = jnp.zeros((ny, nz), jnp.float32)
    smooth = jnp.zeros((ny, nz), jnp.float32)
    for y in range(ny):
        metric = jnp.where(row == y, metric_ref[y], metric)
        smooth = jnp.where(row == y, smooth_ref[y], smooth)
    rate = 1.0 / (CX * smooth)
    decay = jnp.exp(-rate)
    ratio = jnp.exp(-n * rate)
    c = None
    for k in range(n):
        term = jnp.exp(-(2.0 * k + 1.0) * rate)
        c = term if c is None else c + term
    downstream = (G - 1 - i).astype(jnp.float32)
    geo_here = expm1(-2.0 * n * downstream * rate) / expm1(-2.0 * n * rate)
    low = jnp.where(g == 0, 2.0 * metric_ref[0], 0.0)
    high = jnp.where(g == Gy - 1, -2.0 * metric_ref[ny - 1], 0.0)
    shrink = expm1(-rate)
    rows = (metric, decay, c * ratio * geo_here, rate, shrink * shrink, 1.0 / metric,
            jnp.broadcast_to(low, (ny, nz)), jnp.broadcast_to(high, (ny, nz)), c * geo_here, ratio)
    for k, v in enumerate(rows):
        coef_ref[k] = v


def sweep_kernel(adj_ref, base_ref, coef_ref, sw_ref, pay_ref):
    n, ny, nz = adj_ref.shape[1], adj_ref.shape[2], adj_ref.shape[3]
    metric = column(coef_ref, 0, ny, nz)
    decay = column(coef_ref, 1, ny, nz)
    row = lax.broadcasted_iota(jnp.int32, (ny, nz), 0)
    zero = jnp.zeros((ny, nz), jnp.float32)

    def field(k, x):
        if x < 0 or x >= n:
            return zero
        return adj_ref[k, x] if k < 3 else base_ref[k - 3, x]

    forward = [None] * 3
    for x in range(n):
        grads = []
        for k in range(6):
            cur = field(k, x)
            dx = 0.5 * (field(k, x + 1) - field(k, x - 1))
            up = jnp.where(row == ny - 1, 0.0, pltpu.roll(cur, ny - 1, 0))
            down = jnp.where(row == 0, 0.0, pltpu.roll(cur, 1, 0))
            dy = metric * (up - down)
            dz = 0.5 * (pltpu.roll(cur, nz - 1, 1) - pltpu.roll(cur, 1, 1))
            grads.append((dx, dy, dz))
        adj = [field(d, x) for d in range(3)]
        base = [field(3 + d, x) for d in range(3)]
        for c in range(3):
            running = None
            for d in range(3):
                term = -(base[d] * grads[c][d])
                running = term if running is None else running + term
                running = running + adj[d] * grads[3 + d][c]
            inc = step_size * running
            forward[c] = inc if x == 0 else inc + decay * forward[c]
            sw_ref[c, x] = forward[c]
    back = [None] * 3
    for x in range(n - 1, -1, -1):
        for c in range(3):
            f = sw_ref[c, x]
            back[c] = f if x == n - 1 else f + decay * back[c]
            sw_ref[c, x] = back[c]
    for c in range(3):
        pay_ref[0, c] = forward[c]
        pay_ref[1, c] = back[c]


def delta_terms(own, halo, scale, along):
    out = []
    for c in range(3):
        term = -(own[3 + along] * (scale * halo[c]))
        if c == along:
            for d in range(3):
                term = term + own[d] * (scale * halo[3 + d])
        out.append(step_size * term)
    return out


def edge_kernel(sxa_ref, sxb_ref, sya_ref, syb_ref, rxa_ref, rxb_ref, rya_ref, ryb_ref, coef_ref, pre_ref,
                pay_ref, plane_ref, rows_ref):
    n, nz = sya_ref.shape[1], sya_ref.shape[2]
    ny = sxa_ref.shape[1]
    even_x = lax.axis_index("gx") % 2 == 0
    even_y = lax.axis_index("gy") % 2 == 0

    def sort(even, a_ref, b_ref):
        return [jnp.where(even, b_ref[k], a_ref[k]) for k in range(6)], [
            jnp.where(even, a_ref[k], b_ref[k]) for k in range(6)
        ]

    own_xlo, own_xhi = sort(even_x, sxa_ref, sxb_ref)
    own_ylo, own_yhi = sort(even_y, sya_ref, syb_ref)
    before_x, after_x = sort(even_x, rxa_ref, rxb_ref)
    before_y, after_y = sort(even_y, rya_ref, ryb_ref)
    decay = column(coef_ref, 1, ny, nz)
    gain = column(coef_ref, 2, ny, nz)
    rate = column(coef_ref, 3, ny, nz)
    metric = column(coef_ref, 0, ny, nz)
    row = lax.broadcasted_iota(jnp.int32, (ny, nz), 0)
    first = delta_terms(own_xlo, before_x, -0.5, 0)
    last = delta_terms(own_xhi, after_x, 0.5, 0)
    low = delta_terms(own_ylo, before_y, -metric[0:1, :], 1)
    high = delta_terms(own_yhi, after_y, metric[ny - 1 : ny, :], 1)
    d_low = decay[0:1, :]
    d_high = decay[ny - 1 : ny, :]
    reach = jnp.exp(-(n - 1.0) * rate)
    spread = None
    for x in range(n - 1, -1, -1):
        lead = jnp.exp(-x * rate)
        spread = lead if spread is None else lead + decay * spread
    for c in range(3):
        plane_ref[0, c] = first[c]
        plane_ref[1, c] = last[c]
        f_lo = f_hi = None
        fl, fh = [], []
        for x in range(n):
            a = low[c][x : x + 1, :]
            b = high[c][x : x + 1, :]
            f_lo = a if f_lo is None else a + d_low * f_lo
            f_hi = b if f_hi is None else b + d_high * f_hi
            fl.append(f_lo)
            fh.append(f_hi)
        b_lo = b_hi = None
        for x in range(n - 1, -1, -1):
            b_lo = fl[x] if b_lo is None else fl[x] + d_low * b_lo
            b_hi = fh[x] if b_hi is None else fh[x] + d_high * b_hi
            rows_ref[c, 0, x : x + 1, :] = b_lo
            rows_ref[c, 1, x : x + 1, :] = b_hi
        row_l = jnp.where(row == 0, fl[n - 1], 0.0) + jnp.where(row == ny - 1, fh[n - 1], 0.0)
        row_s = jnp.where(row == 0, b_lo, 0.0) + jnp.where(row == ny - 1, b_hi, 0.0)
        carry_up = pre_ref[0, c] + reach * first[c] + last[c] + row_l
        start = pre_ref[1, c] + spread * first[c] + reach * last[c] + row_s
        pay_ref[0, c] = carry_up
        pay_ref[1, c] = start + gain * carry_up


def finish_kernel(G, direct, adj_ref, sw_ref, pay_ref, coef_ref, plane_ref, rows_ref, *rest):
    n, ny, nz = adj_ref.shape[1], adj_ref.shape[2], adj_ref.shape[3]
    out_ref, part_ref = rest[-2], rest[-1]
    got = rest[:-2]
    rate = column(coef_ref, 3, ny, nz)
    decay = column(coef_ref, 1, ny, nz)
    shrink = column(coef_ref, 4, ny, nz)
    inverse = column(coef_ref, 5, ny, nz)
    low_w = column(coef_ref, 6, ny, nz)
    high_w = column(coef_ref, 7, ny, nz)
    near = column(coef_ref, 8, ny, nz)
    ratio = column(coef_ref, 9, ny, nz)
    block_rate = n * rate
    i = lax.axis_index("gx")
    inflow, later = [], []
    if direct:
        pair_ref = got[0]
        far = got[1:]
        odd = (i % 2) == 1
        pair = i // 2
        step_w = jnp.exp(-block_rate)
        weights = []
        for m in range(1, G // 2):
            other = lax.bitwise_xor(pair, jnp.int32(m))
            upstream = other < pair
            power = (jnp.maximum(pair - other, other - pair) - 1).astype(jnp.float32)
            weights.append((upstream, jnp.exp(-2.0 * power * block_rate)))
    for c in range(3):
        if direct:
            a = jnp.zeros_like(rate)
            b = jnp.zeros_like(rate)
            for m in range(1, G // 2):
                upstream, w = weights[m - 1]
                a = a + jnp.where(upstream, w * far[m - 1][0, c], 0.0)
                b = b + jnp.where(upstream, 0.0, w * far[m - 1][1, c])
            a = jnp.where(odd, step_w * a + pair_ref[0, c], a)
            b = jnp.where(odd, b, pair_ref[1, c] + step_w * b)
        else:
            a = got[0][c]
            b = got[1][c]
        inflow.append(a)
        later.append(b + near * (pay_ref[0, c] + ratio * a))
    row = lax.broadcasted_iota(jnp.int32, (ny, nz), 0)
    back_lead = None
    spread = None
    for x in range(n - 1, -1, -1):
        lead = jnp.exp(-(x + 1.0) * rate)
        back_lead = lead if back_lead is None else lead + decay * back_lead
        own_lead = jnp.exp(-x * rate)
        spread = own_lead if spread is None else own_lead + decay * spread
        tail = jnp.exp(-(n - x) * rate)
        reach = jnp.exp(-(n - 1.0 - x) * rate)
        vals = []
        for c in range(3):
            fix = jnp.where(row == 0, rows_ref[c, 0, x : x + 1, :], 0.0) + jnp.where(
                row == ny - 1, rows_ref[c, 1, x : x + 1, :], 0.0
            )
            local = sw_ref[c, x] + spread * plane_ref[0, c] + reach * plane_ref[1, c] + fix
            v = adj_ref[c, x] + shrink * (local + back_lead * inflow[c] + tail * later[c])
            out_ref[c, x] = v
            vals.append(v)
        part_ref[0, x : x + 1, :] = (low_w * vals[1])[0:1, :]
        part_ref[1, x : x + 1, :] = (high_w * vals[1])[ny - 1 : ny, :]
        part_ref[2, x : x + 1, :] = jnp.sum(vals[0] * inverse, axis=0, keepdims=True)
    part_ref[3] = jnp.broadcast_to(jnp.sum(inverse, axis=0, keepdims=True), part_ref.shape[1:])


def swap_pairs(size, phase):
    pairs = []
    for j in range(size):
        mate = j ^ 1 if phase == 0 else (j + 1 if j % 2 else j - 1)
        if 0 <= mate < size:
            pairs.append((j, mate))
    return pairs


def scan_carries(L, U, A, G):
    inflow = shift(L, "gx", G, 1)
    later = shift(U, "gx", G, -1)
    step = 1
    ratio = A
    while step < G:
        inflow = inflow + ratio * shift(inflow, "gx", G, step)
        later = later + ratio * shift(later, "gx", G, -step)
        ratio = ratio * ratio
        step *= 2
    return inflow, later


def local(adjoint, base_flow, metric, smoothing):
    G, i = lax.axis_size("gx"), lax.axis_index("gx")
    Gy, g = lax.axis_size("gy"), lax.axis_index("gy")
    _, n, ny, nz = adjoint.shape

    smem = pl.BlockSpec(memory_space=pltpu.SMEM)
    sxa, sxb, sya, syb, coef = pl.pallas_call(
        edges_kernel,
        out_shape=(f32((6, ny, nz)), f32((6, ny, nz)), f32((6, n, nz)), f32((6, n, nz)), f32((10, ny, nz))),
        in_specs=[smem, smem, pl.BlockSpec(), pl.BlockSpec()],
    )(metric, smoothing, adjoint, base_flow)
    rxa = lax.ppermute(sxa, "gx", swap_pairs(G, 0))
    rxb = lax.ppermute(sxb, "gx", swap_pairs(G, 1))
    rya = lax.ppermute(sya, "gy", swap_pairs(Gy, 0))
    ryb = lax.ppermute(syb, "gy", swap_pairs(Gy, 1))

    sw, pre = pl.pallas_call(
        sweep_kernel,
        out_shape=(f32(adjoint.shape), f32((2, 3, ny, nz))),
    )(adjoint, base_flow, coef)
    payload, plane, rows = pl.pallas_call(
        edge_kernel,
        out_shape=(f32((2, 3, ny, nz)), f32((2, 3, ny, nz)), f32((3, 2, n, nz))),
    )(sxa, sxb, sya, syb, rxa, rxb, rya, ryb, coef, pre)

    direct = 2 <= G <= DIRECT_LIMIT and is_pow2(G)
    if direct:
        mate = lax.ppermute(payload, "gx", [(j, j ^ 1) for j in range(G)])
        odd = (i % 2) == 1
        A = coef[9][None]
        first_l = jnp.where(odd, mate[0], payload[0])
        second_l = jnp.where(odd, payload[0], mate[0])
        first_u = jnp.where(odd, mate[1], payload[1])
        second_u = jnp.where(odd, payload[1], mate[1])
        pair_sum = jnp.stack([A * first_l + second_l, first_u + A * second_u])
        got = [mate] + [
            lax.ppermute(pair_sum, "gx", [(j, j ^ (2 * m)) for j in range(G)]) for m in range(1, G // 2)
        ]
    else:
        A = coef[9]
        got = list(scan_carries(payload[0], payload[1], A[None], G))
    adjoint_next, part = pl.pallas_call(
        lambda *r: finish_kernel(G, direct, *r),
        out_shape=(f32(adjoint.shape), f32((4, n, nz))),
    )(adjoint, sw, payload, coef, plane, rows, *got)

    pieces = [part] + [
        lax.ppermute(part, "gy", [(j, (j + k) % Gy) for j in range(Gy)]) for k in range(1, Gy)
    ]
    stacked = jnp.stack(pieces)
    total = None
    for s in range(Gy):
        piece = lax.dynamic_index_in_dim(stacked, (g - s) % Gy, axis=0, keepdims=False)
        total = piece if total is None else total + piece
    bulk_mean = total[2] / total[3]
    wall_gradient = total[:2] + bulk_mean[None]
    return (adjoint_next, wall_gradient)


def solution(mesh):
    in_specs = (P(None, "gx", "gy", None), P(None, "gx", "gy", None), P("gy"), P("gy"))
    out_specs = (P(None, "gx", "gy", None), P(None, "gx", None))
    return jax.shard_map(local, mesh=mesh, in_specs=in_specs, out_specs=out_specs, check_vma=False)
```

```python
import jax
import jax.numpy as jnp
from jax import lax
from jax.experimental import pallas as pl
from jax.experimental.pallas import tpu as pltpu
from jax.sharding import PartitionSpec as P

step_size = 0.5
CX = 16
DIRECT_LIMIT = 8


def shift(x, axis, size, step):
    if step > 0:
        pairs = [(j, j + step) for j in range(size - step)]
    else:
        pairs = [(j - step, j) for j in range(size + step)]
    return lax.ppermute(x, axis, pairs)


def f32(shape):
    return jax.ShapeDtypeStruct(shape, jnp.float32)


def column(ref, k, ny, nz):
    return ref[k]


def is_pow2(size):
    return size & (size - 1) == 0


def partner_of(j, k, size):
    if is_pow2(size):
        return j ^ k
    return (j + k) % size


def slot_of(g, s, size):
    if is_pow2(size):
        return g ^ s
    return (g - s) % size


def expm1(x):
    t = jnp.ones_like(x)
    for k in range(12, 1, -1):
        t = 1.0 + x * t / k
    return jnp.where(jnp.abs(x) < 0.5, x * t, jnp.exp(x) - 1.0)


def edges_kernel(metric_ref, smooth_ref, adj_ref, base_ref, xa_ref, xb_ref, ya_ref, yb_ref, coef_ref):
    n, ny, nz = adj_ref.shape[1], adj_ref.shape[2], adj_ref.shape[3]
    even_x = lax.axis_index("gx") % 2 == 0
    even_y = lax.axis_index("gy") % 2 == 0
    for k in range(6):
        ref, c = (adj_ref, k) if k < 3 else (base_ref, k - 3)
        lo, hi = ref[c, 0], ref[c, n - 1]
        xa_ref[k] = jnp.where(even_x, hi, lo)
        xb_ref[k] = jnp.where(even_x, lo, hi)
        for x in range(n):
            lo, hi = ref[c, x, 0:1, :], ref[c, x, ny - 1 : ny, :]
            ya_ref[k, x : x + 1, :] = jnp.where(even_y, hi, lo)
            yb_ref[k, x : x + 1, :] = jnp.where(even_y, lo, hi)
    G, i = lax.axis_size("gx"), lax.axis_index("gx")
    Gy, g = lax.axis_size("gy"), lax.axis_index("gy")
    row = lax.broadcasted_iota(jnp.int32, (ny, nz), 0)
    metric = jnp.zeros((ny, nz), jnp.float32)
    smooth = jnp.zeros((ny, nz), jnp.float32)
    for y in range(ny):
        metric = jnp.where(row == y, metric_ref[y], metric)
        smooth = jnp.where(row == y, smooth_ref[y], smooth)
    rate = 1.0 / (CX * smooth)
    decay = jnp.exp(-rate)
    ratio = jnp.exp(-n * rate)
    c = None
    for k in range(n):
        term = jnp.exp(-(2.0 * k + 1.0) * rate)
        c = term if c is None else c + term
    downstream = (G - 1 - i).astype(jnp.float32)
    geo_here = expm1(-2.0 * n * downstream * rate) / expm1(-2.0 * n * rate)
    low = jnp.where(g == 0, 2.0 * metric_ref[0], 0.0)
    high = jnp.where(g == Gy - 1, -2.0 * metric_ref[ny - 1], 0.0)
    shrink = expm1(-rate)
    rows = (metric, decay, c * ratio * geo_here, rate, shrink * shrink, 1.0 / metric,
            jnp.broadcast_to(low, (ny, nz)), jnp.broadcast_to(high, (ny, nz)), c * geo_here, ratio)
    for k, v in enumerate(rows):
        coef_ref[k] = v


def sweep_kernel(adj_ref, base_ref, coef_ref, sw_ref, pay_ref):
    n, ny, nz = adj_ref.shape[1], adj_ref.shape[2], adj_ref.shape[3]
    metric = column(coef_ref, 0, ny, nz)
    decay = column(coef_ref, 1, ny, nz)
    row = lax.broadcasted_iota(jnp.int32, (ny, nz), 0)
    zero = jnp.zeros((ny, nz), jnp.float32)

    def field(k, x):
        if x < 0 or x >= n:
            return zero
        return adj_ref[k, x] if k < 3 else base_ref[k - 3, x]

    forward = [None] * 3
    for x in range(n):
        grads = []
        for k in range(6):
            cur = field(k, x)
            dx = 0.5 * (field(k, x + 1) - field(k, x - 1))
            up = jnp.where(row == ny - 1, 0.0, pltpu.roll(cur, ny - 1, 0))
            down = jnp.where(row == 0, 0.0, pltpu.roll(cur, 1, 0))
            dy = metric * (up - down)
            dz = 0.5 * (pltpu.roll(cur, nz - 1, 1) - pltpu.roll(cur, 1, 1))
            grads.append((dx, dy, dz))
        adj = [field(d, x) for d in range(3)]
        base = [field(3 + d, x) for d in range(3)]
        for c in range(3):
            running = None
            for d in range(3):
                term = -(base[d] * grads[c][d])
                running = term if running is None else running + term
                running = running + adj[d] * grads[3 + d][c]
            inc = step_size * running
            forward[c] = inc if x == 0 else inc + decay * forward[c]
            sw_ref[c, x] = forward[c]
    back = [None] * 3
    for x in range(n - 1, -1, -1):
        for c in range(3):
            f = sw_ref[c, x]
            back[c] = f if x == n - 1 else f + decay * back[c]
            sw_ref[c, x] = back[c]
    for c in range(3):
        pay_ref[0, c] = forward[c]
        pay_ref[1, c] = back[c]


def delta_terms(own, halo, scale, along):
    out = []
    for c in range(3):
        term = -(own[3 + along] * (scale * halo[c]))
        if c == along:
            for d in range(3):
                term = term + own[d] * (scale * halo[3 + d])
        out.append(step_size * term)
    return out


def edge_kernel(sxa_ref, sxb_ref, sya_ref, syb_ref, rxa_ref, rxb_ref, rya_ref, ryb_ref, coef_ref, pre_ref,
                pay_ref, plane_ref, rows_ref):
    n, nz = sya_ref.shape[1], sya_ref.shape[2]
    ny = sxa_ref.shape[1]
    even_x = lax.axis_index("gx") % 2 == 0
    even_y = lax.axis_index("gy") % 2 == 0

    def sort(even, a_ref, b_ref):
        return [jnp.where(even, b_ref[k], a_ref[k]) for k in range(6)], [
            jnp.where(even, a_ref[k], b_ref[k]) for k in range(6)
        ]

    own_xlo, own_xhi = sort(even_x, sxa_ref, sxb_ref)
    own_ylo, own_yhi = sort(even_y, sya_ref, syb_ref)
    before_x, after_x = sort(even_x, rxa_ref, rxb_ref)
    before_y, after_y = sort(even_y, rya_ref, ryb_ref)
    decay = column(coef_ref, 1, ny, nz)
    gain = column(coef_ref, 2, ny, nz)
    rate = column(coef_ref, 3, ny, nz)
    metric = column(coef_ref, 0, ny, nz)
    row = lax.broadcasted_iota(jnp.int32, (ny, nz), 0)
    first = delta_terms(own_xlo, before_x, -0.5, 0)
    last = delta_terms(own_xhi, after_x, 0.5, 0)
    low = delta_terms(own_ylo, before_y, -metric[0:1, :], 1)
    high = delta_terms(own_yhi, after_y, metric[ny - 1 : ny, :], 1)
    d_low = decay[0:1, :]
    d_high = decay[ny - 1 : ny, :]
    reach = jnp.exp(-(n - 1.0) * rate)
    spread = None
    for x in range(n - 1, -1, -1):
        lead = jnp.exp(-x * rate)
        spread = lead if spread is None else lead + decay * spread
    for c in range(3):
        plane_ref[0, c] = first[c]
        plane_ref[1, c] = last[c]
        f_lo = f_hi = None
        fl, fh = [], []
        for x in range(n):
            a = low[c][x : x + 1, :]
            b = high[c][x : x + 1, :]
            f_lo = a if f_lo is None else a + d_low * f_lo
            f_hi = b if f_hi is None else b + d_high * f_hi
            fl.append(f_lo)
            fh.append(f_hi)
        b_lo = b_hi = None
        for x in range(n - 1, -1, -1):
            b_lo = fl[x] if b_lo is None else fl[x] + d_low * b_lo
            b_hi = fh[x] if b_hi is None else fh[x] + d_high * b_hi
            rows_ref[c, 0, x : x + 1, :] = b_lo
            rows_ref[c, 1, x : x + 1, :] = b_hi
        row_l = jnp.where(row == 0, fl[n - 1], 0.0) + jnp.where(row == ny - 1, fh[n - 1], 0.0)
        row_s = jnp.where(row == 0, b_lo, 0.0) + jnp.where(row == ny - 1, b_hi, 0.0)
        carry_up = pre_ref[0, c] + reach * first[c] + last[c] + row_l
        start = pre_ref[1, c] + spread * first[c] + reach * last[c] + row_s
        pay_ref[0, c] = carry_up
        pay_ref[1, c] = start + gain * carry_up


def finish_kernel(G, direct, adj_ref, sw_ref, pay_ref, coef_ref, plane_ref, rows_ref, *rest):
    n, ny, nz = adj_ref.shape[1], adj_ref.shape[2], adj_ref.shape[3]
    out_ref, part_ref = rest[-2], rest[-1]
    got = rest[:-2]
    rate = column(coef_ref, 3, ny, nz)
    decay = column(coef_ref, 1, ny, nz)
    shrink = column(coef_ref, 4, ny, nz)
    inverse = column(coef_ref, 5, ny, nz)
    low_w = column(coef_ref, 6, ny, nz)
    high_w = column(coef_ref, 7, ny, nz)
    near = column(coef_ref, 8, ny, nz)
    ratio = column(coef_ref, 9, ny, nz)
    block_rate = n * rate
    i = lax.axis_index("gx")
    inflow, later = [], []
    if direct:
        pair_ref = got[0]
        far = got[1:]
        odd = (i % 2) == 1
        pair = i // 2
        step_w = jnp.exp(-block_rate)
        weights = []
        for m in range(1, G // 2):
            other = lax.bitwise_xor(pair, jnp.int32(m))
            upstream = other < pair
            power = (jnp.maximum(pair - other, other - pair) - 1).astype(jnp.float32)
            weights.append((upstream, jnp.exp(-2.0 * power * block_rate)))
    for c in range(3):
        if direct:
            a = jnp.zeros_like(rate)
            b = jnp.zeros_like(rate)
            for m in range(1, G // 2):
                upstream, w = weights[m - 1]
                a = a + jnp.where(upstream, w * far[m - 1][0, c], 0.0)
                b = b + jnp.where(upstream, 0.0, w * far[m - 1][1, c])
            a = jnp.where(odd, step_w * a + pair_ref[0, c], a)
            b = jnp.where(odd, b, pair_ref[1, c] + step_w * b)
        else:
            a = got[0][c]
            b = got[1][c]
        inflow.append(a)
        later.append(b + near * (pay_ref[0, c] + ratio * a))
    row = lax.broadcasted_iota(jnp.int32, (ny, nz), 0)
    back_lead = None
    spread = None
    for x in range(n - 1, -1, -1):
        lead = jnp.exp(-(x + 1.0) * rate)
        back_lead = lead if back_lead is None else lead + decay * back_lead
        own_lead = jnp.exp(-x * rate)
        spread = own_lead if spread is None else own_lead + decay * spread
        tail = jnp.exp(-(n - x) * rate)
        reach = jnp.exp(-(n - 1.0 - x) * rate)
        vals = []
        for c in range(3):
            fix = jnp.where(row == 0, rows_ref[c, 0, x : x + 1, :], 0.0) + jnp.where(
                row == ny - 1, rows_ref[c, 1, x : x + 1, :], 0.0
            )
            local = sw_ref[c, x] + spread * plane_ref[0, c] + reach * plane_ref[1, c] + fix
            v = adj_ref[c, x] + shrink * (local + back_lead * inflow[c] + tail * later[c])
            out_ref[c, x] = v
            vals.append(v)
        part_ref[0, x : x + 1, :] = (low_w * vals[1])[0:1, :]
        part_ref[1, x : x + 1, :] = (high_w * vals[1])[ny - 1 : ny, :]
        part_ref[2, x : x + 1, :] = jnp.sum(vals[0] * inverse, axis=0, keepdims=True)
    part_ref[3] = jnp.broadcast_to(jnp.sum(inverse, axis=0, keepdims=True), part_ref.shape[1:])


def swap_pairs(size, phase):
    pairs = []
    for j in range(size):
        mate = j ^ 1 if phase == 0 else (j + 1 if j % 2 else j - 1)
        if 0 <= mate < size:
            pairs.append((j, mate))
    return pairs


def scan_carries(L, U, A, G):
    inflow = shift(L, "gx", G, 1)
    later = shift(U, "gx", G, -1)
    step = 1
    ratio = A
    while step < G:
        inflow = inflow + ratio * shift(inflow, "gx", G, step)
        later = later + ratio * shift(later, "gx", G, -step)
        ratio = ratio * ratio
        step *= 2
    return inflow, later


def local(adjoint, base_flow, metric, smoothing):
    G, i = lax.axis_size("gx"), lax.axis_index("gx")
    Gy, g = lax.axis_size("gy"), lax.axis_index("gy")
    _, n, ny, nz = adjoint.shape

    smem = pl.BlockSpec(memory_space=pltpu.SMEM)
    sxa, sxb, sya, syb, coef = pl.pallas_call(
        edges_kernel,
        out_shape=(f32((6, ny, nz)), f32((6, ny, nz)), f32((6, n, nz)), f32((6, n, nz)), f32((10, ny, nz))),
        in_specs=[smem, smem, pl.BlockSpec(), pl.BlockSpec()],
    )(metric, smoothing, adjoint, base_flow)
    rxa = lax.ppermute(sxa, "gx", swap_pairs(G, 0))
    rxb = lax.ppermute(sxb, "gx", swap_pairs(G, 1))
    rya = lax.ppermute(sya, "gy", swap_pairs(Gy, 0))
    ryb = lax.ppermute(syb, "gy", swap_pairs(Gy, 1))

    sw, pre = pl.pallas_call(
        sweep_kernel,
        out_shape=(f32(adjoint.shape), f32((2, 3, ny, nz))),
    )(adjoint, base_flow, coef)
    payload, plane, rows = pl.pallas_call(
        edge_kernel,
        out_shape=(f32((2, 3, ny, nz)), f32((2, 3, ny, nz)), f32((3, 2, n, nz))),
    )(sxa, sxb, sya, syb, rxa, rxb, rya, ryb, coef, pre)

    direct = 2 <= G <= DIRECT_LIMIT and is_pow2(G)
    if direct:
        mate = lax.ppermute(payload, "gx", [(j, j ^ 1) for j in range(G)])
        odd = (i % 2) == 1
        A = coef[9][None]
        first_l = jnp.where(odd, mate[0], payload[0])
        second_l = jnp.where(odd, payload[0], mate[0])
        first_u = jnp.where(odd, mate[1], payload[1])
        second_u = jnp.where(odd, payload[1], mate[1])
        pair_sum = jnp.stack([A * first_l + second_l, first_u + A * second_u])
        got = [mate] + [
            lax.ppermute(pair_sum, "gx", [(j, j ^ (2 * m)) for j in range(G)]) for m in range(1, G // 2)
        ]
    else:
        A = coef[9]
        got = list(scan_carries(payload[0], payload[1], A[None], G))
    adjoint_next, part = pl.pallas_call(
        lambda *r: finish_kernel(G, direct, *r),
        out_shape=(f32(adjoint.shape), f32((4, n, nz))),
    )(adjoint, sw, payload, coef, plane, rows, *got)

    pieces = [part] + [
        lax.ppermute(part, "gy", [(j, partner_of(j, k, Gy)) for j in range(Gy)]) for k in range(1, Gy)
    ]
    stacked = jnp.stack(pieces)
    total = None
    for s in range(Gy):
        piece = lax.dynamic_index_in_dim(stacked, slot_of(g, s, Gy), axis=0, keepdims=False)
        total = piece if total is None else total + piece
    bulk_mean = total[2] / total[3]
    wall_gradient = total[:2] + bulk_mean[None]
    return (adjoint_next, wall_gradient)


def solution(mesh):
    in_specs = (P(None, "gx", "gy", None), P(None, "gx", "gy", None), P("gy"), P("gy"))
    out_specs = (P(None, "gx", "gy", None), P(None, "gx", None))
    return jax.shard_map(local, mesh=mesh, in_specs=in_specs, out_specs=out_specs, check_vma=False)
```

```python
import jax
import jax.numpy as jnp
from jax import lax
from jax.experimental import pallas as pl
from jax.experimental.pallas import tpu as pltpu
from jax.sharding import PartitionSpec as P

step_size = 0.5
CX = 16
DIRECT_LIMIT = 8


def shift(x, axis, size, step):
    if step > 0:
        pairs = [(j, j + step) for j in range(size - step)]
    else:
        pairs = [(j - step, j) for j in range(size + step)]
    return lax.ppermute(x, axis, pairs)


def f32(shape):
    return jax.ShapeDtypeStruct(shape, jnp.float32)


def column(ref, k, ny, nz):
    return ref[k]


def is_pow2(size):
    return size & (size - 1) == 0


def partner_of(j, k, size):
    if is_pow2(size):
        return j ^ k
    return (j + k) % size


def slot_of(g, s, size):
    if is_pow2(size):
        return g ^ s
    return (g - s) % size


def expm1(x):
    t = jnp.ones_like(x)
    for k in range(12, 1, -1):
        t = 1.0 + x * t / k
    return jnp.where(jnp.abs(x) < 0.5, x * t, jnp.exp(x) - 1.0)


def edges_kernel(metric_ref, smooth_ref, adj_ref, base_ref, xa_ref, xb_ref, ya_ref, yb_ref, coef_ref):
    n, ny, nz = adj_ref.shape[1], adj_ref.shape[2], adj_ref.shape[3]
    even_x = lax.axis_index("gx") % 2 == 0
    even_y = lax.axis_index("gy") % 2 == 0
    for k in range(6):
        ref, c = (adj_ref, k) if k < 3 else (base_ref, k - 3)
        lo, hi = ref[c, 0], ref[c, n - 1]
        xa_ref[k] = jnp.where(even_x, hi, lo)
        xb_ref[k] = jnp.where(even_x, lo, hi)
        for x in range(n):
            lo, hi = ref[c, x, 0:1, :], ref[c, x, ny - 1 : ny, :]
            ya_ref[k, x : x + 1, :] = jnp.where(even_y, hi, lo)
            yb_ref[k, x : x + 1, :] = jnp.where(even_y, lo, hi)
    G, i = lax.axis_size("gx"), lax.axis_index("gx")
    Gy, g = lax.axis_size("gy"), lax.axis_index("gy")
    row = lax.broadcasted_iota(jnp.int32, (ny, nz), 0)
    metric = jnp.zeros((ny, nz), jnp.float32)
    smooth = jnp.zeros((ny, nz), jnp.float32)
    for y in range(ny):
        metric = jnp.where(row == y, metric_ref[y], metric)
        smooth = jnp.where(row == y, smooth_ref[y], smooth)
    rate = 1.0 / (CX * smooth)
    decay = jnp.exp(-rate)
    ratio = jnp.exp(-n * rate)
    c = None
    for k in range(n):
        term = jnp.exp(-(2.0 * k + 1.0) * rate)
        c = term if c is None else c + term
    downstream = (G - 1 - i).astype(jnp.float32)
    geo_here = expm1(-2.0 * n * downstream * rate) / expm1(-2.0 * n * rate)
    low = jnp.where(g == 0, 2.0 * metric_ref[0], 0.0)
    high = jnp.where(g == Gy - 1, -2.0 * metric_ref[ny - 1], 0.0)
    shrink = expm1(-rate)
    rows = (metric, decay, c * ratio * geo_here, rate, shrink * shrink, 1.0 / metric,
            jnp.broadcast_to(low, (ny, nz)), jnp.broadcast_to(high, (ny, nz)), c * geo_here, ratio)
    for k, v in enumerate(rows):
        coef_ref[k] = v


def sweep_kernel(adj_ref, base_ref, coef_ref, sw_ref, pay_ref):
    n, ny, nz = adj_ref.shape[1], adj_ref.shape[2], adj_ref.shape[3]
    metric = column(coef_ref, 0, ny, nz)
    decay = column(coef_ref, 1, ny, nz)
    row = lax.broadcasted_iota(jnp.int32, (ny, nz), 0)
    zero = jnp.zeros((ny, nz), jnp.float32)

    def field(k, x):
        if x < 0 or x >= n:
            return zero
        return adj_ref[k, x] if k < 3 else base_ref[k - 3, x]

    forward = [None] * 3
    for x in range(n):
        grads = []
        for k in range(6):
            cur = field(k, x)
            dx = 0.5 * (field(k, x + 1) - field(k, x - 1))
            up = jnp.where(row == ny - 1, 0.0, pltpu.roll(cur, ny - 1, 0))
            down = jnp.where(row == 0, 0.0, pltpu.roll(cur, 1, 0))
            dy = metric * (up - down)
            dz = 0.5 * (pltpu.roll(cur, nz - 1, 1) - pltpu.roll(cur, 1, 1))
            grads.append((dx, dy, dz))
        adj = [field(d, x) for d in range(3)]
        base = [field(3 + d, x) for d in range(3)]
        for c in range(3):
            running = None
            for d in range(3):
                term = -(base[d] * grads[c][d])
                running = term if running is None else running + term
                running = running + adj[d] * grads[3 + d][c]
            inc = step_size * running
            forward[c] = inc if x == 0 else inc + decay * forward[c]
            sw_ref[c, x] = forward[c]
    back = [None] * 3
    for x in range(n - 1, -1, -1):
        for c in range(3):
            f = sw_ref[c, x]
            back[c] = f if x == n - 1 else f + decay * back[c]
            sw_ref[c, x] = back[c]
    for c in range(3):
        pay_ref[0, c] = forward[c]
        pay_ref[1, c] = back[c]


def delta_terms(own, halo, scale, along):
    out = []
    for c in range(3):
        term = -(own[3 + along] * (scale * halo[c]))
        if c == along:
            for d in range(3):
                term = term + own[d] * (scale * halo[3 + d])
        out.append(step_size * term)
    return out


def edge_kernel(sxa_ref, sxb_ref, sya_ref, syb_ref, rxa_ref, rxb_ref, rya_ref, ryb_ref, coef_ref, pre_ref,
                pay_ref, plane_ref, rows_ref):
    n, nz = sya_ref.shape[1], sya_ref.shape[2]
    ny = sxa_ref.shape[1]
    even_x = lax.axis_index("gx") % 2 == 0
    even_y = lax.axis_index("gy") % 2 == 0

    def sort(even, a_ref, b_ref):
        return [jnp.where(even, b_ref[k], a_ref[k]) for k in range(6)], [
            jnp.where(even, a_ref[k], b_ref[k]) for k in range(6)
        ]

    own_xlo, own_xhi = sort(even_x, sxa_ref, sxb_ref)
    own_ylo, own_yhi = sort(even_y, sya_ref, syb_ref)
    before_x, after_x = sort(even_x, rxa_ref, rxb_ref)
    before_y, after_y = sort(even_y, rya_ref, ryb_ref)
    decay = column(coef_ref, 1, ny, nz)
    gain = column(coef_ref, 2, ny, nz)
    rate = column(coef_ref, 3, ny, nz)
    metric = column(coef_ref, 0, ny, nz)
    row = lax.broadcasted_iota(jnp.int32, (ny, nz), 0)
    first = delta_terms(own_xlo, before_x, -0.5, 0)
    last = delta_terms(own_xhi, after_x, 0.5, 0)
    low = delta_terms(own_ylo, before_y, -metric[0:1, :], 1)
    high = delta_terms(own_yhi, after_y, metric[ny - 1 : ny, :], 1)
    d_low = decay[0:1, :]
    d_high = decay[ny - 1 : ny, :]
    reach = jnp.exp(-(n - 1.0) * rate)
    spread = None
    for x in range(n - 1, -1, -1):
        lead = jnp.exp(-x * rate)
        spread = lead if spread is None else lead + decay * spread
    for c in range(3):
        plane_ref[0, c] = first[c]
        plane_ref[1, c] = last[c]
        f_lo = f_hi = None
        fl, fh = [], []
        for x in range(n):
            a = low[c][x : x + 1, :]
            b = high[c][x : x + 1, :]
            f_lo = a if f_lo is None else a + d_low * f_lo
            f_hi = b if f_hi is None else b + d_high * f_hi
            fl.append(f_lo)
            fh.append(f_hi)
        b_lo = b_hi = None
        for x in range(n - 1, -1, -1):
            b_lo = fl[x] if b_lo is None else fl[x] + d_low * b_lo
            b_hi = fh[x] if b_hi is None else fh[x] + d_high * b_hi
            rows_ref[c, 0, x : x + 1, :] = b_lo
            rows_ref[c, 1, x : x + 1, :] = b_hi
        row_l = jnp.where(row == 0, fl[n - 1], 0.0) + jnp.where(row == ny - 1, fh[n - 1], 0.0)
        row_s = jnp.where(row == 0, b_lo, 0.0) + jnp.where(row == ny - 1, b_hi, 0.0)
        carry_up = pre_ref[0, c] + reach * first[c] + last[c] + row_l
        start = pre_ref[1, c] + spread * first[c] + reach * last[c] + row_s
        pay_ref[0, c] = carry_up
        pay_ref[1, c] = start + gain * carry_up


def finish_kernel(G, direct, adj_ref, sw_ref, pay_ref, coef_ref, plane_ref, rows_ref, *rest):
    n, ny, nz = adj_ref.shape[1], adj_ref.shape[2], adj_ref.shape[3]
    out_ref, part_ref = rest[-2], rest[-1]
    got = rest[:-2]
    rate = column(coef_ref, 3, ny, nz)
    decay = column(coef_ref, 1, ny, nz)
    shrink = column(coef_ref, 4, ny, nz)
    inverse = column(coef_ref, 5, ny, nz)
    low_w = column(coef_ref, 6, ny, nz)
    high_w = column(coef_ref, 7, ny, nz)
    near = column(coef_ref, 8, ny, nz)
    ratio = column(coef_ref, 9, ny, nz)
    block_rate = n * rate
    i = lax.axis_index("gx")
    inflow, later = [], []
    if direct:
        pair_ref = got[0]
        far = got[1:]
        odd = (i % 2) == 1
        pair = i // 2
        step_w = jnp.exp(-block_rate)
        weights = []
        for m in range(1, G // 2):
            other = lax.bitwise_xor(pair, jnp.int32(m))
            upstream = other < pair
            power = (jnp.maximum(pair - other, other - pair) - 1).astype(jnp.float32)
            weights.append((upstream, jnp.exp(-2.0 * power * block_rate)))
    for c in range(3):
        if direct:
            a = jnp.zeros_like(rate)
            b = jnp.zeros_like(rate)
            for m in range(1, G // 2):
                upstream, w = weights[m - 1]
                a = a + jnp.where(upstream, w * far[m - 1][0, c], 0.0)
                b = b + jnp.where(upstream, 0.0, w * far[m - 1][1, c])
            a = jnp.where(odd, step_w * a + pair_ref[0, c], a)
            b = jnp.where(odd, b, pair_ref[1, c] + step_w * b)
        else:
            a = got[0][c]
            b = got[1][c]
        inflow.append(a)
        later.append(b + near * (pay_ref[0, c] + ratio * a))
    row = lax.broadcasted_iota(jnp.int32, (ny, nz), 0)
    back_lead = None
    spread = None
    for x in range(n - 1, -1, -1):
        lead = jnp.exp(-(x + 1.0) * rate)
        back_lead = lead if back_lead is None else lead + decay * back_lead
        own_lead = jnp.exp(-x * rate)
        spread = own_lead if spread is None else own_lead + decay * spread
        tail = jnp.exp(-(n - x) * rate)
        reach = jnp.exp(-(n - 1.0 - x) * rate)
        vals = []
        for c in range(3):
            fix = jnp.where(row == 0, rows_ref[c, 0, x : x + 1, :], 0.0) + jnp.where(
                row == ny - 1, rows_ref[c, 1, x : x + 1, :], 0.0
            )
            local = sw_ref[c, x] + spread * plane_ref[0, c] + reach * plane_ref[1, c] + fix
            v = adj_ref[c, x] + shrink * (local + back_lead * inflow[c] + tail * later[c])
            out_ref[c, x] = v
            vals.append(v)
        part_ref[0, x : x + 1, :] = (low_w * vals[1])[0:1, :]
        part_ref[1, x : x + 1, :] = (high_w * vals[1])[ny - 1 : ny, :]
        part_ref[2, x : x + 1, :] = jnp.sum(vals[0] * inverse, axis=0, keepdims=True)
    part_ref[3] = jnp.broadcast_to(jnp.sum(inverse, axis=0, keepdims=True), part_ref.shape[1:])


def swap_pairs(size, phase):
    pairs = []
    for j in range(size):
        mate = j ^ 1 if phase == 0 else (j + 1 if j % 2 else j - 1)
        if 0 <= mate < size:
            pairs.append((j, mate))
    return pairs


def scan_carries(L, U, A, G):
    inflow = shift(L, "gx", G, 1)
    later = shift(U, "gx", G, -1)
    step = 1
    ratio = A
    while step < G:
        inflow = inflow + ratio * shift(inflow, "gx", G, step)
        later = later + ratio * shift(later, "gx", G, -step)
        ratio = ratio * ratio
        step *= 2
    return inflow, later


def local(adjoint, base_flow, metric, smoothing):
    G, i = lax.axis_size("gx"), lax.axis_index("gx")
    Gy, g = lax.axis_size("gy"), lax.axis_index("gy")
    _, n, ny, nz = adjoint.shape

    smem = pl.BlockSpec(memory_space=pltpu.SMEM)
    sxa, sxb, sya, syb, coef = pl.pallas_call(
        edges_kernel,
        out_shape=(f32((6, ny, nz)), f32((6, ny, nz)), f32((6, n, nz)), f32((6, n, nz)), f32((10, ny, nz))),
        in_specs=[smem, smem, pl.BlockSpec(), pl.BlockSpec()],
    )(metric, smoothing, adjoint, base_flow)
    rxa = lax.ppermute(sxa, "gx", swap_pairs(G, 0))
    rxb = lax.ppermute(sxb, "gx", swap_pairs(G, 1))
    rya = lax.ppermute(sya, "gy", swap_pairs(Gy, 0))
    ryb = lax.ppermute(syb, "gy", swap_pairs(Gy, 1))

    sw, pre = pl.pallas_call(
        sweep_kernel,
        out_shape=(f32(adjoint.shape), f32((2, 3, ny, nz))),
    )(adjoint, base_flow, coef)
    payload, plane, rows = pl.pallas_call(
        edge_kernel,
        out_shape=(f32((2, 3, ny, nz)), f32((2, 3, ny, nz)), f32((3, 2, n, nz))),
    )(sxa, sxb, sya, syb, rxa, rxb, rya, ryb, coef, pre)

    direct = 2 <= G <= DIRECT_LIMIT and is_pow2(G)
    if direct:
        mate = lax.ppermute(payload, "gx", [(j, j ^ 1) for j in range(G)])
        odd = (i % 2) == 1
        A = coef[9][None]
        first_l = jnp.where(odd, mate[0], payload[0])
        second_l = jnp.where(odd, payload[0], mate[0])
        first_u = jnp.where(odd, mate[1], payload[1])
        second_u = jnp.where(odd, payload[1], mate[1])
        pair_sum = jnp.stack([A * first_l + second_l, first_u + A * second_u])
        got = [mate] + [
            lax.ppermute(pair_sum, "gx", [(j, j ^ (2 * m)) for j in range(G)]) for m in range(1, G // 2)
        ]
    else:
        A = coef[9]
        got = list(scan_carries(payload[0], payload[1], A[None], G))
    adjoint_next, part = pl.pallas_call(
        lambda *r: finish_kernel(G, direct, *r),
        out_shape=(f32(adjoint.shape), f32((4, n, nz))),
    )(adjoint, sw, payload, coef, plane, rows, *got)

    if is_pow2(Gy):
        total = part
        level = 1
        while level < Gy:
            total = total + lax.ppermute(total, "gy", [(j, j ^ level) for j in range(Gy)])
            level *= 2
    else:
        pieces = [part] + [
            lax.ppermute(part, "gy", [(j, (j + k) % Gy) for j in range(Gy)]) for k in range(1, Gy)
        ]
        stacked = jnp.stack(pieces)
        total = None
        for s in range(Gy):
            piece = lax.dynamic_index_in_dim(stacked, (g - s) % Gy, axis=0, keepdims=False)
            total = piece if total is None else total + piece
    bulk_mean = total[2] / total[3]
    wall_gradient = total[:2] + bulk_mean[None]
    return (adjoint_next, wall_gradient)


def solution(mesh):
    in_specs = (P(None, "gx", "gy", None), P(None, "gx", "gy", None), P("gy"), P("gy"))
    out_specs = (P(None, "gx", "gy", None), P(None, "gx", None))
    return jax.shard_map(local, mesh=mesh, in_specs=in_specs, out_specs=out_specs, check_vma=False)
```
